256 devices in a mesh: tm: 8 (over z), owner: 32 (over y, x, core).
Axes of the slice: x: 4, y: 4, z: 8, core: 2. Of those that a mesh axis runs over, the one named last changes fastest.
Arguments:
- pressure: bfloat16 [512, 262144], P('tm', 'owner'), may hold values from -6 to 6
- proj_weight: bfloat16 [32, 64, 4, 128, 128], P('owner', 'tm'), may hold values from -0.1875 to 0.1875
- pattern: int32 [32, 64, 4], P('owner', 'tm'), may hold values from 0 to 31, as said below
- panel_list: int32 [32, 32], replicated, may hold values from 0 to 767, as said below
- owner_list: int32 [32, 36], replicated, may hold values from -1 to 767, as said below
- owner_count: int32 [32], replicated, may hold values from 12 to 36, as said below
Outputs:
- panel_field: float32 [1152, 512, 128], P('owner', 'tm')
The draws below stay inside these ranges and needn't reach their ends.
Inputs may be any that keep to these rules, and one draw needn't show every extreme that they name: `pattern`: the 4 entries of one face block are different. `panel_list`: each row names different panel blocks, owned by 16 different owners, exactly 2 of each. `owner_list`: slots below an owner's count hold its panel blocks; every panel block stands in exactly one such slot; slots from the count on hold -1. `owner_count`: the counts sum to 768.
All inputs are finite; a program needn't handle non-finite values.
Results may differ from the reference program's by a relative error of at most 0.0003.
Values may be sent and summed in bfloat16 or wider, within the bound.
No kernel may reach another device: no remote copies, remote signals or barrier semaphores. Data moves between devices by JAX's collectives and lax.ppermute only.
A program may use at most 128 MiB of HBM per device.

```python
import jax
import jax.numpy as jnp
from jax import lax

TIME = 512
BLOCK = 128
KP = 4
FB_DEV = 8
LP = 32
PB_OWN = 24
SLOT = 2
CAP = 36
PANELS = 768
FB_SHARD = 64
FACES = 262144
N_TM = 8
N_OWNER = 32


def ownership(key):
    owner_order = jax.random.permutation(jax.random.fold_in(key, 101), N_OWNER)
    spread = CAP - PB_OWN
    offsets = jax.random.randint(jax.random.fold_in(key, 102), (N_OWNER // 2,), 0, spread + 1)
    offsets = jnp.where(jnp.arange(N_OWNER // 2) == 0, spread, offsets)
    paired = jnp.stack([PB_OWN + offsets, PB_OWN - offsets], axis=1).reshape(-1).astype(jnp.int32)
    counts = jnp.zeros((N_OWNER,), jnp.int32).at[owner_order].set(paired)
    starts = jnp.cumsum(counts) - counts
    shuffled = jax.random.permutation(jax.random.fold_in(key, 103), PB_OWN * N_OWNER).astype(jnp.int32)
    column = jnp.arange(CAP, dtype=jnp.int32)
    position = jnp.minimum(starts[:, None] + column[None, :], PB_OWN * N_OWNER - 1)
    listed = jnp.where(column[None, :] < counts[:, None], shuffled[position], -1)
    return (listed.astype(jnp.int32), counts)


def draw_owner_list(key, part):
    listed, counts = ownership(key)
    return listed


def draw_owner_count(key, part):
    listed, counts = ownership(key)
    return counts


def draw_panel_list(key, part):
    listed, counts = ownership(key)
    groups = LP // SLOT
    rotation = jax.random.randint(jax.random.fold_in(key, 201), (N_OWNER, 1), 0, N_OWNER)
    chosen = (jnp.arange(N_OWNER)[:, None] + rotation + jnp.arange(groups)[None, :]) % N_OWNER
    first_slot = jax.random.randint(jax.random.fold_in(key, 202), (N_OWNER, groups), 0, counts[chosen])
    within = jnp.arange(LP) % SLOT
    member = jnp.arange(LP) // SLOT
    owner_rows = chosen[:, member]
    placing = (first_slot[:, member] + within[None, :]) % counts[owner_rows]
    panels = listed[owner_rows, placing]
    row_keys = jax.random.split(jax.random.fold_in(key, 203), N_OWNER)
    return jax.vmap(jax.random.permutation)(row_keys, panels).astype(jnp.int32)


def draw_pattern(key, part):
    row_count = N_OWNER * N_TM * FB_DEV
    row_keys = jax.random.split(jax.random.fold_in(key, 301), row_count)
    chosen_slots = jax.vmap(lambda row_key: jax.random.permutation(row_key, LP)[:KP])(row_keys)
    return chosen_slots.reshape(N_OWNER, N_TM * FB_DEV, KP).astype(jnp.int32)


def levels(own_key, extent, cuts, smallest, largest):
    loudness, own = 1.0, jax.random.fold_in(own_key, 6)
    for axis_at, parts in cuts:
        heights = jnp.exp(jax.random.uniform(jax.random.fold_in(own, axis_at), (parts,), jnp.float32, smallest / len(cuts), largest / len(cuts)))
        loudness = loudness * jnp.repeat(heights, extent[axis_at] // parts).reshape([-1 if axis == axis_at else 1 for axis in range(len(extent))])
    return loudness


def scatter_about(rng, extent, scale, reach, pieces=(), kind=jnp.bfloat16):
    loudness = levels(rng, extent, pieces, -0.22, 0.18) if pieces else 1.0
    drawn = jax.random.normal(rng, extent, jnp.float32) * scale * loudness
    return jnp.minimum(jnp.maximum(drawn, -reach), reach).astype(kind)


def setup_inputs(seed: int = 0) -> dict:
    seeds = jax.random.split(jax.random.key(seed), 7)
    return {
        "pressure": scatter_about(seeds[0], (TIME, FACES), 1.0, 6.0, ((0, 8), (1, 32))),
        "proj_weight": scatter_about(seeds[1], (N_OWNER, FB_SHARD, KP, BLOCK, BLOCK), (BLOCK * FB_SHARD * KP // LP) ** -0.5, 0.1875, ((0, 32), (1, 8))),
        "pattern": draw_pattern(jax.random.fold_in(seeds[6], 71), 0),
        "panel_list": draw_panel_list(jax.random.fold_in(seeds[6], 71), 0),
        "owner_list": draw_owner_list(jax.random.fold_in(seeds[6], 71), 0),
        "owner_count": draw_owner_count(jax.random.fold_in(seeds[6], 71), 0),
    }


def reference(pressure, proj_weight, pattern, panel_list, owner_list, owner_count):
    face_ids = jnp.arange(FB_SHARD, dtype=jnp.int32)

    def shard_step(totals, shard_index):
        weights = proj_weight[shard_index]
        targets = pattern[shard_index]

        def face_step(partial_value, item):
            face_index, weight_rows, target_rows = item
            start = (shard_index * FB_SHARD + face_index) * BLOCK
            face_rows = lax.dynamic_slice_in_dim(pressure, start.astype(jnp.int32), BLOCK, 1)
            contrib = jnp.einsum('ta,kab->ktb', face_rows.astype(jnp.float32), weight_rows.astype(jnp.float32))
            return partial_value.at[target_rows].add(contrib), None

        partial_value, _ = lax.scan(face_step, jnp.zeros((LP, TIME, BLOCK), jnp.float32), (face_ids, weights, targets))
        return totals.at[panel_list[shard_index]].add(partial_value), None

    totals, _ = lax.scan(shard_step, jnp.zeros((PANELS, TIME, BLOCK), jnp.float32), jnp.arange(N_OWNER, dtype=jnp.int32))
    live_slots = jnp.arange(CAP, dtype=jnp.int32)[None, :] < owner_count[:, None]
    picked = totals[jnp.where(live_slots, owner_list, 0)]
    result = jnp.where(live_slots[:, :, None, None], picked, jnp.zeros_like(picked))
    return result.reshape(N_OWNER * CAP, TIME, BLOCK)
```

```python
import functools

import jax
import jax.numpy as jnp
from jax import lax
from jax.experimental import pallas as pl
from jax.experimental.pallas import tpu as pltpu
from jax.sharding import PartitionSpec as P


def send_positions(panel_list, owner_list, owner_count, own_index, slot_count):
    owner_size, capacity = owner_list.shape
    row = panel_list[own_index]
    list_len = row.shape[0]
    live = jnp.arange(capacity, dtype=jnp.int32)[None, :] < owner_count[:, None]
    match = (row[:, None, None] == owner_list[None, :, :]) & live[None, :, :]
    owned_by = jnp.any(match, axis=2)
    owner_of = jnp.sum(jnp.where(owned_by, jnp.arange(owner_size, dtype=jnp.int32)[None, :], 0), axis=1)
    position = jnp.arange(list_len, dtype=jnp.int32)
    earlier = (owner_of[:, None] == owner_of[None, :]) & (position[None, :] < position[:, None])
    rank = jnp.sum(earlier.astype(jnp.int32), axis=1)
    return owner_of * slot_count + rank


def receive_slots(panel_list, owner_list, owner_count, own_index, slot_count):
    capacity = owner_list.shape[1]
    list_len = panel_list.shape[1]
    wanted = owner_list[own_index]
    live = jnp.arange(capacity, dtype=jnp.int32) < owner_count[own_index]
    match = (panel_list[:, :, None] == wanted[None, None, :]) & live[None, None, :]
    hit = jnp.any(match, axis=2)
    slot_of = jnp.sum(jnp.where(match, jnp.arange(capacity, dtype=jnp.int32)[None, None, :], 0), axis=2)
    position = jnp.arange(list_len, dtype=jnp.int32)
    earlier = hit[:, None, :] & (position[None, None, :] < position[None, :, None])
    rank = jnp.sum(earlier.astype(jnp.int32), axis=2)
    ranks = jnp.arange(slot_count, dtype=jnp.int32)
    chosen = hit[:, :, None] & (rank[:, :, None] == ranks[None, None, :])
    found = jnp.any(chosen, axis=1)
    dest = jnp.sum(jnp.where(chosen, slot_of[:, :, None], 0), axis=1)
    return jnp.where(found, dest, capacity).reshape(-1)


def project_kernel(group, kp, block_len, idx_ref, p_ref, w_ref, o_ref):
    step = pl.program_id(0)

    @pl.when(step == 0)
    def _():
        o_ref[...] = jnp.zeros_like(o_ref)

    for g in range(group):
        rows = p_ref[:, g * block_len:(g + 1) * block_len]
        for k in range(kp):
            pos = idx_ref[(step * group + g) * kp + k]
            o_ref[pos] += jnp.dot(rows, w_ref[g, k], preferred_element_type=jnp.float32)


def project(idx, pressure, weights, n_pos, group=8):
    fb, kp, block_len, _ = weights.shape
    time_len = pressure.shape[0]
    steps = fb // group
    return pl.pallas_call(
        functools.partial(project_kernel, group, kp, block_len),
        out_shape=jax.ShapeDtypeStruct((n_pos, time_len, block_len), jnp.float32),
        grid_spec=pltpu.PrefetchScalarGridSpec(
            num_scalar_prefetch=1,
            grid=(steps,),
            in_specs=[
                pl.BlockSpec((time_len, group * block_len), lambda c, idx: (0, c)),
                pl.BlockSpec((group, kp, block_len, block_len), lambda c, idx: (c, 0, 0, 0)),
            ],
            out_specs=pl.BlockSpec((n_pos, time_len, block_len), lambda c, idx: (0, 0, 0)),
        ),
        compiler_params=pltpu.CompilerParams(dimension_semantics=("arbitrary",)),
        cost_estimate=pl.CostEstimate(
            flops=2 * fb * kp * time_len * block_len * block_len,
            bytes_accessed=weights.size * 2 + pressure.size * 2 + n_pos * time_len * block_len * 4,
            transcendentals=0,
        ),
    )(idx, pressure, weights)


def collect_kernel(n_rows, dest_ref, r_ref, o_ref, acc_ref):
    acc_ref[...] = jnp.zeros_like(acc_ref)

    def add_row(e, carry):
        d = dest_ref[e]
        acc_ref[d] += r_ref[e]
        return carry

    lax.fori_loop(0, n_rows, add_row, 0)
    o_ref[...] = acc_ref[: o_ref.shape[0]]


def collect(dest, received, capacity):
    n_rows, time_len, block_len = received.shape
    return pl.pallas_call(
        functools.partial(collect_kernel, n_rows),
        out_shape=jax.ShapeDtypeStruct((capacity, time_len, block_len), jnp.float32),
        in_specs=[
            pl.BlockSpec(memory_space=pltpu.SMEM),
            pl.BlockSpec(memory_space=pltpu.VMEM),
        ],
        out_specs=pl.BlockSpec(memory_space=pltpu.VMEM),
        scratch_shapes=[pltpu.VMEM((capacity + 1, time_len, block_len), jnp.float32)],
    )(dest, received)


def body(pressure, proj_weight, pattern, panel_list, owner_list, owner_count):
    owner_size = lax.axis_size("owner")
    own_index = lax.axis_index("owner")
    list_len = panel_list.shape[1]
    capacity = owner_list.shape[1]
    slot_count = max(2, list_len // owner_size)
    n_pos = owner_size * slot_count

    weights = lax.all_gather(proj_weight[0], "tm", axis=0, tiled=True)
    positions = send_positions(panel_list, owner_list, owner_count, own_index, slot_count)
    local_idx = jnp.take(positions, pattern[0], axis=0)
    idx = lax.all_gather(local_idx, "tm", axis=0, tiled=True).reshape(-1)

    packed = project(idx, pressure, weights, n_pos)
    received = lax.all_to_all(packed, "owner", split_axis=0, concat_axis=0, tiled=True)
    dest = receive_slots(panel_list, owner_list, owner_count, own_index, slot_count)
    return collect(dest, received, capacity)


def solution(mesh):
    placed = (
        P("tm", "owner"),
        P("owner", "tm", None, None, None),
        P("owner", "tm", None),
        P(),
        P(),
        P(),
    )
    return jax.shard_map(
        body, mesh=mesh, in_specs=placed, out_specs=P("owner", "tm", None), check_vma=False
    )
```

```python
import functools

import jax
import jax.numpy as jnp
from jax import lax
from jax.experimental import pallas as pl
from jax.experimental.pallas import tpu as pltpu
from jax.sharding import PartitionSpec as P


def send_positions(panel_list, owner_list, owner_count, own_index, slot_count):
    owner_size, capacity = owner_list.shape
    row = panel_list[own_index]
    list_len = row.shape[0]
    live = jnp.arange(capacity, dtype=jnp.int32)[None, :] < owner_count[:, None]
    match = (row[:, None, None] == owner_list[None, :, :]) & live[None, :, :]
    owned_by = jnp.any(match, axis=2)
    owner_of = jnp.sum(jnp.where(owned_by, jnp.arange(owner_size, dtype=jnp.int32)[None, :], 0), axis=1)
    position = jnp.arange(list_len, dtype=jnp.int32)
    earlier = (owner_of[:, None] == owner_of[None, :]) & (position[None, :] < position[:, None])
    rank = jnp.sum(earlier.astype(jnp.int32), axis=1)
    return owner_of * slot_count + rank


def receive_slots(panel_list, owner_list, owner_count, own_index, slot_count):
    capacity = owner_list.shape[1]
    list_len = panel_list.shape[1]
    wanted = owner_list[own_index]
    live = jnp.arange(capacity, dtype=jnp.int32) < owner_count[own_index]
    match = (panel_list[:, :, None] == wanted[None, None, :]) & live[None, None, :]
    hit = jnp.any(match, axis=2)
    slot_of = jnp.sum(jnp.where(match, jnp.arange(capacity, dtype=jnp.int32)[None, None, :], 0), axis=2)
    position = jnp.arange(list_len, dtype=jnp.int32)
    earlier = hit[:, None, :] & (position[None, None, :] < position[None, :, None])
    rank = jnp.sum(earlier.astype(jnp.int32), axis=2)
    ranks = jnp.arange(slot_count, dtype=jnp.int32)
    chosen = hit[:, :, None] & (rank[:, :, None] == ranks[None, None, :])
    found = jnp.any(chosen, axis=1)
    dest = jnp.sum(jnp.where(chosen, slot_of[:, :, None], 0), axis=1)
    return jnp.where(found, dest, capacity).reshape(-1)


def project_kernel(group, kp, block_len, first, idx_ref, off_ref, p_ref, w_ref, *refs):
    if first:
        (o_ref,) = refs
        o_ref[...] = jnp.zeros_like(o_ref)
    else:
        acc_ref, o_ref = refs
        o_ref[...] = acc_ref[...]
    for g in range(group):
        rows = p_ref[:, g * block_len:(g + 1) * block_len]
        for k in range(kp):
            pos = idx_ref[g * kp + k]
            o_ref[pos] += jnp.dot(rows, w_ref[g, k], preferred_element_type=jnp.float32)


def project(idx, block_at, pressure, weights, acc, n_pos):
    group, kp, block_len, _ = weights.shape
    time_len = pressure.shape[0]
    first = acc is None
    out_block = pl.BlockSpec((n_pos, time_len, block_len), lambda c, idx, off: (0, 0, 0))
    in_specs = [
        pl.BlockSpec((time_len, group * block_len), lambda c, idx, off: (0, off[0])),
        pl.BlockSpec((group, kp, block_len, block_len), lambda c, idx, off: (0, 0, 0, 0)),
    ]
    operands = [idx, jnp.reshape(block_at, (1,)).astype(jnp.int32), pressure, weights]
    aliases = {}
    if not first:
        in_specs.append(out_block)
        operands.append(acc)
        aliases = {4: 0}
    return pl.pallas_call(
        functools.partial(project_kernel, group, kp, block_len, first),
        out_shape=jax.ShapeDtypeStruct((n_pos, time_len, block_len), jnp.float32),
        grid_spec=pltpu.PrefetchScalarGridSpec(
            num_scalar_prefetch=2,
            grid=(1,),
            in_specs=in_specs,
            out_specs=out_block,
        ),
        input_output_aliases=aliases,
        cost_estimate=pl.CostEstimate(
            flops=2 * group * kp * time_len * block_len * block_len,
            bytes_accessed=weights.size * 2 + time_len * group * block_len * 2
            + 2 * n_pos * time_len * block_len * 4,
            transcendentals=0,
        ),
    )(*operands)


def collect_kernel(n_rows, dest_ref, r_ref, o_ref, acc_ref):
    acc_ref[...] = jnp.zeros_like(acc_ref)

    def add_row(e, carry):
        d = dest_ref[e]
        acc_ref[d] += r_ref[e]
        return carry

    lax.fori_loop(0, n_rows, add_row, 0)
    o_ref[...] = acc_ref[: o_ref.shape[0]]


def collect(dest, received, capacity):
    n_rows, time_len, block_len = received.shape
    return pl.pallas_call(
        functools.partial(collect_kernel, n_rows),
        out_shape=jax.ShapeDtypeStruct((capacity, time_len, block_len), jnp.float32),
        in_specs=[
            pl.BlockSpec(memory_space=pltpu.SMEM),
            pl.BlockSpec(memory_space=pltpu.VMEM),
        ],
        out_specs=pl.BlockSpec(memory_space=pltpu.VMEM),
        scratch_shapes=[pltpu.VMEM((capacity + 1, time_len, block_len), jnp.float32)],
    )(dest, received)


def body(pressure, proj_weight, pattern, panel_list, owner_list, owner_count):
    owner_size = lax.axis_size("owner")
    own_index = lax.axis_index("owner")
    list_len = panel_list.shape[1]
    capacity = owner_list.shape[1]
    slot_count = max(2, list_len // owner_size)
    n_pos = owner_size * slot_count

    n_tm = lax.axis_size("tm")
    t = lax.axis_index("tm")
    positions = send_positions(panel_list, owner_list, owner_count, own_index, slot_count)
    right = [(i, (i + 1) % n_tm) for i in range(n_tm)]
    left = [(i, (i - 1) % n_tm) for i in range(n_tm)]

    def chunk(weights, pat, block_at, acc):
        idx = jnp.take(positions, pat, axis=0).reshape(-1)
        return project(idx, block_at, pressure, weights, acc, n_pos)

    w_r = w_l = proj_weight[0]
    p_r = p_l = pattern[0]
    packed = chunk(w_r, p_r, t, None)
    for s in range(1, n_tm // 2):
        w_r, p_r = lax.ppermute((w_r, p_r), "tm", right)
        w_l, p_l = lax.ppermute((w_l, p_l), "tm", left)
        packed = chunk(w_r, p_r, (t - s) % n_tm, packed)
        packed = chunk(w_l, p_l, (t + s) % n_tm, packed)
    half = w_r.shape[0] // 2
    far = (t + n_tm // 2) % n_tm
    h_r, q_r = lax.ppermute((w_r[:half], p_r[:half]), "tm", right)
    h_l, q_l = lax.ppermute((w_l[half:], p_l[half:]), "tm", left)
    packed = chunk(h_r, q_r, 2 * far, packed)
    packed = chunk(h_l, q_l, 2 * far + 1, packed)
    received = lax.all_to_all(packed, "owner", split_axis=0, concat_axis=0, tiled=True)
    dest = receive_slots(panel_list, owner_list, owner_count, own_index, slot_count)
    return collect(dest, received, capacity)


def solution(mesh):
    placed = (
        P("tm", "owner"),
        P("owner", "tm", None, None, None),
        P("owner", "tm", None),
        P(),
        P(),
        P(),
    )
    return jax.shard_map(
        body, mesh=mesh, in_specs=placed, out_specs=P("owner", "tm", None), check_vma=False
    )
```

```python
import functools

import jax
import jax.numpy as jnp
from jax import lax
from jax.experimental import pallas as pl
from jax.experimental.pallas import tpu as pltpu
from jax.sharding import PartitionSpec as P


def send_positions(panel_list, owner_list, owner_count, own_index, slot_count):
    owner_size, capacity = owner_list.shape
    row = panel_list[own_index]
    list_len = row.shape[0]
    live = jnp.arange(capacity, dtype=jnp.int32)[None, :] < owner_count[:, None]
    match = (row[:, None, None] == owner_list[None, :, :]) & live[None, :, :]
    owned_by = jnp.any(match, axis=2)
    owner_of = jnp.sum(jnp.where(owned_by, jnp.arange(owner_size, dtype=jnp.int32)[None, :], 0), axis=1)
    position = jnp.arange(list_len, dtype=jnp.int32)
    earlier = (owner_of[:, None] == owner_of[None, :]) & (position[None, :] < position[:, None])
    rank = jnp.sum(earlier.astype(jnp.int32), axis=1)
    return owner_of * slot_count + rank


def receive_slots(panel_list, owner_list, owner_count, own_index, slot_count):
    capacity = owner_list.shape[1]
    list_len = panel_list.shape[1]
    wanted = owner_list[own_index]
    live = jnp.arange(capacity, dtype=jnp.int32) < owner_count[own_index]
    match = (panel_list[:, :, None] == wanted[None, None, :]) & live[None, None, :]
    hit = jnp.any(match, axis=2)
    slot_of = jnp.sum(jnp.where(match, jnp.arange(capacity, dtype=jnp.int32)[None, None, :], 0), axis=2)
    position = jnp.arange(list_len, dtype=jnp.int32)
    earlier = hit[:, None, :] & (position[None, None, :] < position[None, :, None])
    rank = jnp.sum(earlier.astype(jnp.int32), axis=2)
    ranks = jnp.arange(slot_count, dtype=jnp.int32)
    chosen = hit[:, :, None] & (rank[:, :, None] == ranks[None, None, :])
    found = jnp.any(chosen, axis=1)
    dest = jnp.sum(jnp.where(chosen, slot_of[:, :, None], 0), axis=1)
    return jnp.where(found, dest, capacity).reshape(-1)


def project_kernel(group, kp, block_len, idx_ref, p_ref, w_ref, o_ref):
    step = pl.program_id(0)

    @pl.when(step == 0)
    def _():
        o_ref[...] = jnp.zeros_like(o_ref)

    for g in range(group):
        rows = p_ref[:, g * block_len:(g + 1) * block_len]
        wide = jnp.concatenate([w_ref[g, k] for k in range(kp)], axis=1)
        prod = jnp.dot(rows, wide, preferred_element_type=jnp.float32)
        for k in range(kp):
            pos = idx_ref[(step * group + g) * kp + k]
            o_ref[pos] += prod[:, k * block_len:(k + 1) * block_len]


def project(idx, pressure, weights, n_pos, group=32):
    fb, kp, block_len, _ = weights.shape
    time_len = pressure.shape[0]
    steps = fb // group
    return pl.pallas_call(
        functools.partial(project_kernel, group, kp, block_len),
        out_shape=jax.ShapeDtypeStruct((n_pos, time_len, block_len), jnp.float32),
        grid_spec=pltpu.PrefetchScalarGridSpec(
            num_scalar_prefetch=1,
            grid=(steps,),
            in_specs=[
                pl.BlockSpec((time_len, group * block_len), lambda c, idx: (0, c)),
                pl.BlockSpec((group, kp, block_len, block_len), lambda c, idx: (c, 0, 0, 0)),
            ],
            out_specs=pl.BlockSpec((n_pos, time_len, block_len), lambda c, idx: (0, 0, 0)),
        ),
        compiler_params=pltpu.CompilerParams(dimension_semantics=("arbitrary",)),
        cost_estimate=pl.CostEstimate(
            flops=2 * fb * kp * time_len * block_len * block_len,
            bytes_accessed=weights.size * 2 + pressure.size * 2 + n_pos * time_len * block_len * 4,
            transcendentals=0,
        ),
    )(idx, pressure, weights)


def collect_kernel(n_rows, dest_ref, r_ref, o_ref, acc_ref):
    acc_ref[...] = jnp.zeros_like(acc_ref)

    def add_row(e, carry):
        d = dest_ref[e]
        acc_ref[d] += r_ref[e]
        return carry

    lax.fori_loop(0, n_rows, add_row, 0)
    o_ref[...] = acc_ref[: o_ref.shape[0]]


def collect(dest, received, capacity):
    n_rows, time_len, block_len = received.shape
    return pl.pallas_call(
        functools.partial(collect_kernel, n_rows),
        out_shape=jax.ShapeDtypeStruct((capacity, time_len, block_len), jnp.float32),
        in_specs=[
            pl.BlockSpec(memory_space=pltpu.SMEM),
            pl.BlockSpec(memory_space=pltpu.VMEM),
        ],
        out_specs=pl.BlockSpec(memory_space=pltpu.VMEM),
        scratch_shapes=[pltpu.VMEM((capacity + 1, time_len, block_len), jnp.float32)],
    )(dest, received)


def body(pressure, proj_weight, pattern, panel_list, owner_list, owner_count):
    owner_size = lax.axis_size("owner")
    own_index = lax.axis_index("owner")
    list_len = panel_list.shape[1]
    capacity = owner_list.shape[1]
    slot_count = max(2, list_len // owner_size)
    n_pos = owner_size * slot_count

    weights = lax.all_gather(proj_weight[0], "tm", axis=0, tiled=True)
    positions = send_positions(panel_list, owner_list, owner_count, own_index, slot_count)
    local_idx = jnp.take(positions, pattern[0], axis=0)
    idx = lax.all_gather(local_idx, "tm", axis=0, tiled=True).reshape(-1)

    packed = project(idx, pressure, weights, n_pos)
    received = lax.all_to_all(packed, "owner", split_axis=0, concat_axis=0, tiled=True)
    dest = receive_slots(panel_list, owner_list, owner_count, own_index, slot_count)
    return collect(dest, received, capacity)


def solution(mesh):
    placed = (
        P("tm", "owner"),
        P("owner", "tm", None, None, None),
        P("owner", "tm", None),
        P(),
        P(),
        P(),
    )
    return jax.shard_map(
        body, mesh=mesh, in_specs=placed, out_specs=P("owner", "tm", None), check_vma=False
    )
```

```python
import functools

import jax
import jax.numpy as jnp
from jax import lax
from jax.experimental import pallas as pl
from jax.experimental.pallas import tpu as pltpu
from jax.sharding import PartitionSpec as P


def send_positions(panel_list, owner_list, owner_count, own_index, slot_count):
    owner_size, capacity = owner_list.shape
    row = panel_list[own_index]
    list_len = row.shape[0]
    live = jnp.arange(capacity, dtype=jnp.int32)[None, :] < owner_count[:, None]
    match = (row[:, None, None] == owner_list[None, :, :]) & live[None, :, :]
    owned_by = jnp.any(match, axis=2)
    owner_of = jnp.sum(jnp.where(owned_by, jnp.arange(owner_size, dtype=jnp.int32)[None, :], 0), axis=1)
    position = jnp.arange(list_len, dtype=jnp.int32)
    earlier = (owner_of[:, None] == owner_of[None, :]) & (position[None, :] < position[:, None])
    rank = jnp.sum(earlier.astype(jnp.int32), axis=1)
    return owner_of * slot_count + rank


def receive_slots(panel_list, owner_list, owner_count, own_index, slot_count):
    capacity = owner_list.shape[1]
    list_len = panel_list.shape[1]
    wanted = owner_list[own_index]
    live = jnp.arange(capacity, dtype=jnp.int32) < owner_count[own_index]
    match = (panel_list[:, :, None] == wanted[None, None, :]) & live[None, None, :]
    hit = jnp.any(match, axis=2)
    slot_of = jnp.sum(jnp.where(match, jnp.arange(capacity, dtype=jnp.int32)[None, None, :], 0), axis=2)
    position = jnp.arange(list_len, dtype=jnp.int32)
    earlier = hit[:, None, :] & (position[None, None, :] < position[None, :, None])
    rank = jnp.sum(earlier.astype(jnp.int32), axis=2)
    ranks = jnp.arange(slot_count, dtype=jnp.int32)
    chosen = hit[:, :, None] & (rank[:, :, None] == ranks[None, None, :])
    found = jnp.any(chosen, axis=1)
    dest = jnp.sum(jnp.where(chosen, slot_of[:, :, None], 0), axis=1)
    return jnp.where(found, dest, capacity).reshape(-1)


def project_kernel(sizes, kp, block_len, idx_ref, blk_ref, p_ref, *refs):
    n = len(sizes)
    w_refs = refs[:n]
    o_ref, buf, sem = refs[n:]
    o_ref[...] = jnp.zeros_like(o_ref)

    def fetch(q):
        slot = q % 2
        return pltpu.make_async_copy(w_refs[q], buf.at[slot, pl.ds(0, sizes[q])], sem.at[slot])

    copies = [fetch(0)]
    copies[0].start()
    base = 0
    for q in range(n):
        copies[q].wait()
        if q + 1 < n:
            copies.append(fetch(q + 1))
            copies[q + 1].start()
        slot = q % 2
        for g in range(sizes[q]):
            col = pl.multiple_of((blk_ref[q] + g) * block_len, block_len)
            rows = p_ref[:, pl.ds(col, block_len)]
            wide = jnp.concatenate([buf[slot, g, k] for k in range(kp)], axis=1)
            prod = jnp.dot(rows, wide, preferred_element_type=jnp.float32)
            for k in range(kp):
                pos = idx_ref[(base + g) * kp + k]
                o_ref[pos] += prod[:, k * block_len:(k + 1) * block_len]
        base += sizes[q]


def project(idx, blk, pressure, pieces, n_pos):
    sizes = tuple(w.shape[0] for w in pieces)
    _, kp, block_len, _ = pieces[0].shape
    time_len = pressure.shape[0]
    face_blocks = sum(sizes)
    return pl.pallas_call(
        functools.partial(project_kernel, sizes, kp, block_len),
        out_shape=jax.ShapeDtypeStruct((n_pos, time_len, block_len), jnp.float32),
        in_specs=[
            pl.BlockSpec(memory_space=pltpu.SMEM),
            pl.BlockSpec(memory_space=pltpu.SMEM),
            pl.BlockSpec(memory_space=pltpu.VMEM),
        ]
        + [pl.BlockSpec(memory_space=pl.ANY)] * len(pieces),
        out_specs=pl.BlockSpec(memory_space=pltpu.VMEM),
        scratch_shapes=[
            pltpu.VMEM((2, max(sizes), kp, block_len, block_len), pieces[0].dtype),
            pltpu.SemaphoreType.DMA((2,)),
        ],
        cost_estimate=pl.CostEstimate(
            flops=2 * face_blocks * kp * time_len * block_len * block_len,
            bytes_accessed=face_blocks * kp * block_len * block_len * 2 + pressure.size * 2
            + n_pos * time_len * block_len * 4,
            transcendentals=0,
        ),
    )(idx, blk, pressure, *pieces)


def collect_kernel(n_rows, dest_ref, r_ref, o_ref, acc_ref):
    acc_ref[...] = jnp.zeros_like(acc_ref)

    def add_row(e, carry):
        d = dest_ref[e]
        acc_ref[d] += r_ref[e]
        return carry

    lax.fori_loop(0, n_rows, add_row, 0)
    o_ref[...] = acc_ref[: o_ref.shape[0]]


def collect(dest, received, capacity):
    n_rows, time_len, block_len = received.shape
    return pl.pallas_call(
        functools.partial(collect_kernel, n_rows),
        out_shape=jax.ShapeDtypeStruct((capacity, time_len, block_len), jnp.float32),
        in_specs=[
            pl.BlockSpec(memory_space=pltpu.SMEM),
            pl.BlockSpec(memory_space=pltpu.VMEM),
        ],
        out_specs=pl.BlockSpec(memory_space=pltpu.VMEM),
        scratch_shapes=[pltpu.VMEM((capacity + 1, time_len, block_len), jnp.float32)],
    )(dest, received)


def body(pressure, proj_weight, pattern, panel_list, owner_list, owner_count):
    owner_size = lax.axis_size("owner")
    own_index = lax.axis_index("owner")
    list_len = panel_list.shape[1]
    capacity = owner_list.shape[1]
    slot_count = max(2, list_len // owner_size)
    n_pos = owner_size * slot_count

    n_tm = lax.axis_size("tm")
    t = lax.axis_index("tm")
    fb_dev = pattern.shape[1]
    right = [(i, (i + 1) % n_tm) for i in range(n_tm)]
    left = [(i, (i - 1) % n_tm) for i in range(n_tm)]

    w_r = w_l = proj_weight[0]
    p_r = p_l = pattern[0]
    pieces, pats, starts = [w_r], [p_r], [t * fb_dev]
    for s in range(1, n_tm // 2):
        w_r, p_r = lax.ppermute((w_r, p_r), "tm", right)
        w_l, p_l = lax.ppermute((w_l, p_l), "tm", left)
        pieces += [w_r, w_l]
        pats += [p_r, p_l]
        starts += [((t - s) % n_tm) * fb_dev, ((t + s) % n_tm) * fb_dev]
    half = fb_dev // 2
    far = (t + n_tm // 2) % n_tm
    h_r, q_r = lax.ppermute((w_r[:half], p_r[:half]), "tm", right)
    h_l, q_l = lax.ppermute((w_l[half:], p_l[half:]), "tm", left)
    pieces += [h_r, h_l]
    pats += [q_r, q_l]
    starts += [far * fb_dev, far * fb_dev + half]

    positions = send_positions(panel_list, owner_list, owner_count, own_index, slot_count)
    idx = jnp.take(positions, jnp.concatenate(pats, axis=0), axis=0).reshape(-1)
    blk = jnp.stack(starts).astype(jnp.int32)
    packed = project(idx, blk, pressure, pieces, n_pos)
    received = lax.all_to_all(packed, "owner", split_axis=0, concat_axis=0, tiled=True)
    dest = receive_slots(panel_list, owner_list, owner_count, own_index, slot_count)
    return collect(dest, received, capacity)


def solution(mesh):
    placed = (
        P("tm", "owner"),
        P("owner", "tm", None, None, None),
        P("owner", "tm", None),
        P(),
        P(),
        P(),
    )
    return jax.shard_map(
        body, mesh=mesh, in_specs=placed, out_specs=P("owner", "tm", None), check_vma=False
    )
```

```python
import functools

import jax
import jax.numpy as jnp
from jax import lax
from jax.experimental import pallas as pl
from jax.experimental.pallas import tpu as pltpu
from jax.sharding import PartitionSpec as P


def send_positions(panel_list, owner_list, owner_count, own_index, slot_count):
    owner_size, capacity = owner_list.shape
    row = panel_list[own_index]
    list_len = row.shape[0]
    live = jnp.arange(capacity, dtype=jnp.int32)[None, :] < owner_count[:, None]
    match = (row[:, None, None] == owner_list[None, :, :]) & live[None, :, :]
    owned_by = jnp.any(match, axis=2)
    owner_of = jnp.sum(jnp.where(owned_by, jnp.arange(owner_size, dtype=jnp.int32)[None, :], 0), axis=1)
    position = jnp.arange(list_len, dtype=jnp.int32)
    earlier = (owner_of[:, None] == owner_of[None, :]) & (position[None, :] < position[:, None])
    rank = jnp.sum(earlier.astype(jnp.int32), axis=1)
    return owner_of * slot_count + rank


def receive_slots(panel_list, owner_list, owner_count, own_index, slot_count):
    capacity = owner_list.shape[1]
    list_len = panel_list.shape[1]
    wanted = owner_list[own_index]
    live = jnp.arange(capacity, dtype=jnp.int32) < owner_count[own_index]
    match = (panel_list[:, :, None] == wanted[None, None, :]) & live[None, None, :]
    hit = jnp.any(match, axis=2)
    slot_of = jnp.sum(jnp.where(match, jnp.arange(capacity, dtype=jnp.int32)[None, None, :], 0), axis=2)
    position = jnp.arange(list_len, dtype=jnp.int32)
    earlier = hit[:, None, :] & (position[None, None, :] < position[None, :, None])
    rank = jnp.sum(earlier.astype(jnp.int32), axis=2)
    ranks = jnp.arange(slot_count, dtype=jnp.int32)
    chosen = hit[:, :, None] & (rank[:, :, None] == ranks[None, None, :])
    found = jnp.any(chosen, axis=1)
    dest = jnp.sum(jnp.where(chosen, slot_of[:, :, None], 0), axis=1)
    return jnp.where(found, dest, capacity).reshape(-1)


def project_kernel(sizes, kp, block_len, idx_ref, p_ref, *refs):
    n = len(sizes)
    w_refs = refs[:n]
    o_ref, buf, sem = refs[n:]
    o_ref[...] = jnp.zeros_like(o_ref)

    def fetch(q):
        slot = q % 2
        rows = sizes[q] * kp * block_len
        return pltpu.make_async_copy(
            w_refs[q].at[pl.ds(0, rows)], buf.at[slot, pl.ds(0, rows)], sem.at[slot]
        )

    copies = [fetch(0)]
    copies[0].start()
    base = 0
    for q in range(n):
        copies[q].wait()
        if q + 1 < n:
            copies.append(fetch(q + 1))
            copies[q + 1].start()
        slot = q % 2
        for g in range(sizes[q]):
            face = base + g
            rows = p_ref[:, face * block_len:(face + 1) * block_len]
            wide = jnp.concatenate(
                [buf[slot, (g * kp + k) * block_len:(g * kp + k + 1) * block_len, :] for k in range(kp)],
                axis=1,
            )
            prod = jnp.dot(rows, wide, preferred_element_type=jnp.float32)
            for k in range(kp):
                pos = idx_ref[face * kp + k]
                o_ref[pos] += prod[:, k * block_len:(k + 1) * block_len]
        base += sizes[q]


def project(idx, pressure, pieces, sizes, kp, n_pos):
    time_len, block_len = pressure.shape[0], pieces[0].shape[1]
    face_blocks = sum(sizes)
    return pl.pallas_call(
        functools.partial(project_kernel, tuple(sizes), kp, block_len),
        out_shape=jax.ShapeDtypeStruct((n_pos, time_len, block_len), jnp.float32),
        in_specs=[
            pl.BlockSpec(memory_space=pltpu.SMEM),
            pl.BlockSpec(memory_space=pltpu.VMEM),
        ]
        + [pl.BlockSpec(memory_space=pl.ANY)] * len(pieces),
        out_specs=pl.BlockSpec(memory_space=pltpu.VMEM),
        scratch_shapes=[
            pltpu.VMEM((2, max(sizes) * kp * block_len, block_len), pieces[0].dtype),
            pltpu.SemaphoreType.DMA((2,)),
        ],
        cost_estimate=pl.CostEstimate(
            flops=2 * face_blocks * kp * time_len * block_len * block_len,
            bytes_accessed=face_blocks * kp * block_len * block_len * 2 + pressure.size * 2
            + n_pos * time_len * block_len * 4,
            transcendentals=0,
        ),
    )(idx, pressure, *pieces)


def collect_kernel(n_rows, dest_ref, r_ref, o_ref, acc_ref):
    acc_ref[...] = jnp.zeros_like(acc_ref)

    def add_row(e, carry):
        d = dest_ref[e]
        acc_ref[d] += r_ref[e]
        return carry

    lax.fori_loop(0, n_rows, add_row, 0)
    o_ref[...] = acc_ref[: o_ref.shape[0]]


def collect(dest, received, capacity):
    n_rows, time_len, block_len = received.shape
    return pl.pallas_call(
        functools.partial(collect_kernel, n_rows),
        out_shape=jax.ShapeDtypeStruct((capacity, time_len, block_len), jnp.float32),
        in_specs=[
            pl.BlockSpec(memory_space=pltpu.SMEM),
            pl.BlockSpec(memory_space=pltpu.VMEM),
        ],
        out_specs=pl.BlockSpec(memory_space=pltpu.VMEM),
        scratch_shapes=[pltpu.VMEM((capacity + 1, time_len, block_len), jnp.float32)],
    )(dest, received)


def body(pressure, proj_weight, pattern, panel_list, owner_list, owner_count):
    owner_size = lax.axis_size("owner")
    own_index = lax.axis_index("owner")
    list_len = panel_list.shape[1]
    capacity = owner_list.shape[1]
    slot_count = max(2, list_len // owner_size)
    n_pos = owner_size * slot_count

    n_tm = lax.axis_size("tm")
    t = lax.axis_index("tm")
    fb_dev, kp, block_len = proj_weight.shape[1], proj_weight.shape[2], proj_weight.shape[3]
    half = fb_dev // 2
    w_rows = fb_dev * kp * block_len
    right = [(i, (i + 1) % n_tm) for i in range(n_tm)]
    left = [(i, (i - 1) % n_tm) for i in range(n_tm)]

    pat_row = jnp.zeros((1, block_len), proj_weight.dtype)
    pat_row = pat_row.at[0, : fb_dev * kp].set(pattern[0].reshape(-1).astype(proj_weight.dtype))
    own = jnp.concatenate([proj_weight[0].reshape(w_rows, block_len), pat_row], axis=0)

    x_r = x_l = own
    pieces, sizes, lane_at, order = [own], [fb_dev], [0], [t]
    for s in range(1, n_tm // 2):
        x_r = lax.ppermute(x_r, "tm", right)
        x_l = lax.ppermute(x_l, "tm", left)
        pieces += [x_r, x_l]
        sizes += [fb_dev, fb_dev]
        lane_at += [0, 0]
        order += [(t - s) % n_tm, (t + s) % n_tm]
    h_rows = half * kp * block_len
    h_r = lax.ppermute(jnp.concatenate([x_r[:h_rows], x_r[w_rows:]], axis=0), "tm", right)
    h_l = lax.ppermute(x_l[h_rows:], "tm", left)
    pieces += [h_r, h_l]
    sizes += [half, half]
    lane_at += [0, half * kp]
    order += [(t + n_tm // 2) % n_tm]

    positions = send_positions(panel_list, owner_list, owner_count, own_index, slot_count)
    pats = [x[-1, a:a + n * kp] for x, n, a in zip(pieces, sizes, lane_at)]
    pat_all = jnp.concatenate(pats).astype(jnp.int32)
    idx = jnp.take(positions, pat_all, axis=0)
    time_len = pressure.shape[0]
    blocks = pressure.reshape(time_len, n_tm, fb_dev * block_len)
    ordered = jnp.take(blocks, jnp.stack(order), axis=1).reshape(time_len, -1)
    packed = project(idx, ordered, pieces, sizes, kp, n_pos)
    received = lax.all_to_all(packed, "owner", split_axis=0, concat_axis=0, tiled=True)
    dest = receive_slots(panel_list, owner_list, owner_count, own_index, slot_count)
    return collect(dest, received, capacity)


def solution(mesh):
    placed = (
        P("tm", "owner"),
        P("owner", "tm", None, None, None),
        P("owner", "tm", None),
        P(),
        P(),
        P(),
    )
    return jax.shard_map(
        body, mesh=mesh, in_specs=placed, out_specs=P("owner", "tm", None), check_vma=False
    )
```

```python
import functools

import jax
import jax.numpy as jnp
from jax import lax
from jax.experimental import pallas as pl
from jax.experimental.pallas import tpu as pltpu
from jax.sharding import PartitionSpec as P


def send_positions(panel_list, owner_list, owner_count, own_index, slot_count):
    owner_size, capacity = owner_list.shape
    row = panel_list[own_index]
    list_len = row.shape[0]
    live = jnp.arange(capacity, dtype=jnp.int32)[None, :] < owner_count[:, None]
    match = (row[:, None, None] == owner_list[None, :, :]) & live[None, :, :]
    owned_by = jnp.any(match, axis=2)
    owner_of = jnp.sum(jnp.where(owned_by, jnp.arange(owner_size, dtype=jnp.int32)[None, :], 0), axis=1)
    position = jnp.arange(list_len, dtype=jnp.int32)
    earlier = (owner_of[:, None] == owner_of[None, :]) & (position[None, :] < position[:, None])
    rank = jnp.sum(earlier.astype(jnp.int32), axis=1)
    return owner_of * slot_count + rank


def receive_slots(panel_list, owner_list, owner_count, own_index, slot_count):
    capacity = owner_list.shape[1]
    list_len = panel_list.shape[1]
    wanted = owner_list[own_index]
    live = jnp.arange(capacity, dtype=jnp.int32) < owner_count[own_index]
    match = (panel_list[:, :, None] == wanted[None, None, :]) & live[None, None, :]
    hit = jnp.any(match, axis=2)
    slot_of = jnp.sum(jnp.where(match, jnp.arange(capacity, dtype=jnp.int32)[None, None, :], 0), axis=2)
    position = jnp.arange(list_len, dtype=jnp.int32)
    earlier = hit[:, None, :] & (position[None, None, :] < position[None, :, None])
    rank = jnp.sum(earlier.astype(jnp.int32), axis=2)
    ranks = jnp.arange(slot_count, dtype=jnp.int32)
    chosen = hit[:, :, None] & (rank[:, :, None] == ranks[None, None, :])
    found = jnp.any(chosen, axis=1)
    dest = jnp.sum(jnp.where(chosen, slot_of[:, :, None], 0), axis=1)
    return jnp.where(found, dest, capacity).reshape(-1)


def project_kernel(sizes, kp, block_len, face_base, has_acc, pos_ref, pat_ref, p_ref, *refs):
    n = len(sizes)
    w_refs = refs[:n]
    if has_acc:
        acc_ref, o_ref, buf, sem = refs[n:]
        o_ref[...] = acc_ref[...]
    else:
        o_ref, buf, sem = refs[n:]
        o_ref[...] = jnp.zeros_like(o_ref)

    def fetch(q):
        slot = q % 2
        rows = sizes[q] * kp * block_len
        return pltpu.make_async_copy(
            w_refs[q].at[pl.ds(0, rows)], buf.at[slot, pl.ds(0, rows)], sem.at[slot]
        )

    copies = [fetch(0)]
    copies[0].start()
    base = 0
    for q in range(n):
        copies[q].wait()
        if q + 1 < n:
            copies.append(fetch(q + 1))
            copies[q + 1].start()
        slot = q % 2
        for g in range(sizes[q]):
            face = base + g
            col = face_base + face
            rows = p_ref[:, col * block_len:(col + 1) * block_len]
            wide = jnp.concatenate(
                [buf[slot, (g * kp + k) * block_len:(g * kp + k + 1) * block_len, :] for k in range(kp)],
                axis=1,
            )
            prod = jnp.dot(rows, wide, preferred_element_type=jnp.float32)
            for k in range(kp):
                pos = pos_ref[pat_ref[face * kp + k]]
                o_ref[pos] += prod[:, k * block_len:(k + 1) * block_len]
        base += sizes[q]


def project(positions, pat, pressure, pieces, sizes, kp, n_pos, face_base, acc):
    time_len, block_len = pressure.shape[0], pieces[0].shape[1]
    face_blocks = sum(sizes)
    has_acc = acc is not None
    extra = [acc] if has_acc else []
    return pl.pallas_call(
        functools.partial(project_kernel, tuple(sizes), kp, block_len, face_base, has_acc),
        out_shape=jax.ShapeDtypeStruct((n_pos, time_len, block_len), jnp.float32),
        in_specs=[
            pl.BlockSpec(memory_space=pltpu.SMEM),
            pl.BlockSpec(memory_space=pltpu.SMEM),
            pl.BlockSpec(memory_space=pltpu.VMEM),
        ]
        + [pl.BlockSpec(memory_space=pl.ANY)] * len(pieces)
        + [pl.BlockSpec(memory_space=pltpu.VMEM)] * len(extra),
        out_specs=pl.BlockSpec(memory_space=pltpu.VMEM),
        scratch_shapes=[
            pltpu.VMEM((2, max(sizes) * kp * block_len, block_len), pieces[0].dtype),
            pltpu.SemaphoreType.DMA((2,)),
        ],
        cost_estimate=pl.CostEstimate(
            flops=2 * face_blocks * kp * time_len * block_len * block_len,
            bytes_accessed=face_blocks * kp * block_len * block_len * 2 + pressure.size * 2
            + (1 + len(extra)) * n_pos * time_len * block_len * 4,
            transcendentals=0,
        ),
    )(positions, pat, pressure, *pieces, *extra)


def collect_kernel(n_rows, dest_ref, r_ref, o_ref, acc_ref):
    acc_ref[...] = jnp.zeros_like(acc_ref)

    def add_row(e, carry):
        d = dest_ref[e]
        acc_ref[d] += r_ref[e]
        return carry

    lax.fori_loop(0, n_rows, add_row, 0)
    o_ref[...] = acc_ref[: o_ref.shape[0]]


def collect(dest, received, capacity):
    n_rows, time_len, block_len = received.shape
    return pl.pallas_call(
        functools.partial(collect_kernel, n_rows),
        out_shape=jax.ShapeDtypeStruct((capacity, time_len, block_len), jnp.float32),
        in_specs=[
            pl.BlockSpec(memory_space=pltpu.SMEM),
            pl.BlockSpec(memory_space=pltpu.VMEM),
        ],
        out_specs=pl.BlockSpec(memory_space=pltpu.VMEM),
        scratch_shapes=[pltpu.VMEM((capacity + 1, time_len, block_len), jnp.float32)],
    )(dest, received)


def body(pressure, proj_weight, pattern, panel_list, owner_list, owner_count):
    owner_size = lax.axis_size("owner")
    own_index = lax.axis_index("owner")
    list_len = panel_list.shape[1]
    capacity = owner_list.shape[1]
    slot_count = max(2, list_len // owner_size)
    n_pos = owner_size * slot_count

    n_tm = lax.axis_size("tm")
    t = lax.axis_index("tm")
    fb_dev, kp, block_len = proj_weight.shape[1], proj_weight.shape[2], proj_weight.shape[3]
    half = fb_dev // 2
    w_rows = fb_dev * kp * block_len
    right = [(i, (i + 1) % n_tm) for i in range(n_tm)]
    left = [(i, (i - 1) % n_tm) for i in range(n_tm)]

    pat_row = jnp.zeros((1, block_len), proj_weight.dtype)
    pat_row = pat_row.at[0, : fb_dev * kp].set(pattern[0].reshape(-1).astype(proj_weight.dtype))
    own = jnp.concatenate([proj_weight[0].reshape(w_rows, block_len), pat_row], axis=0)

    x_r = x_l = own
    pieces, sizes, lane_at, order = [own], [fb_dev], [0], [t]
    for s in range(1, n_tm // 2):
        x_r = lax.ppermute(x_r, "tm", right)
        x_l = lax.ppermute(x_l, "tm", left)
        pieces += [x_r, x_l]
        sizes += [fb_dev, fb_dev]
        lane_at += [0, 0]
        order += [(t - s) % n_tm, (t + s) % n_tm]
    h_rows = half * kp * block_len
    h_r = lax.ppermute(jnp.concatenate([x_r[:h_rows], x_r[w_rows:]], axis=0), "tm", right)
    h_l = lax.ppermute(x_l[h_rows:], "tm", left)
    pieces += [h_r, h_l]
    sizes += [half, half]
    lane_at += [0, half * kp]
    order += [(t + n_tm // 2) % n_tm]

    positions = send_positions(panel_list, owner_list, owner_count, own_index, slot_count)
    time_len = pressure.shape[0]
    blocks = pressure.reshape(time_len, n_tm, fb_dev * block_len)
    ordered = jnp.take(blocks, jnp.stack(order), axis=1).reshape(time_len, -1)

    def pattern_of(group):
        rows = [pieces[i][-1, lane_at[i]:lane_at[i] + sizes[i] * kp] for i in group]
        return jnp.concatenate(rows).astype(jnp.int32)

    full = list(range(len(pieces) - 2))
    tail = [len(pieces) - 2, len(pieces) - 1]
    packed = project(positions, pattern_of(full), ordered, [pieces[i] for i in full],
                     [sizes[i] for i in full], kp, n_pos, 0, None)
    packed = project(positions, pattern_of(tail), ordered, [pieces[i] for i in tail],
                     [sizes[i] for i in tail], kp, n_pos, sum(sizes[i] for i in full), packed)
    received = lax.all_to_all(packed, "owner", split_axis=0, concat_axis=0, tiled=True)
    dest = receive_slots(panel_list, owner_list, owner_count, own_index, slot_count)
    return collect(dest, received, capacity)


def solution(mesh):
    placed = (
        P("tm", "owner"),
        P("owner", "tm", None, None, None),
        P("owner", "tm", None),
        P(),
        P(),
        P(),
    )
    return jax.shard_map(
        body, mesh=mesh, in_specs=placed, out_specs=P("owner", "tm", None), check_vma=False
    )
```

```python
import functools

import jax
import jax.numpy as jnp
from jax import lax
from jax.experimental import pallas as pl
from jax.experimental.pallas import tpu as pltpu
from jax.sharding import PartitionSpec as P


def send_positions(panel_list, owner_list, owner_count, own_index, slot_count):
    owner_size, capacity = owner_list.shape
    row = panel_list[own_index]
    list_len = row.shape[0]
    live = jnp.arange(capacity, dtype=jnp.int32)[None, :] < owner_count[:, None]
    match = (row[:, None, None] == owner_list[None, :, :]) & live[None, :, :]
    owned_by = jnp.any(match, axis=2)
    owner_of = jnp.sum(jnp.where(owned_by, jnp.arange(owner_size, dtype=jnp.int32)[None, :], 0), axis=1)
    position = jnp.arange(list_len, dtype=jnp.int32)
    earlier = (owner_of[:, None] == owner_of[None, :]) & (position[None, :] < position[:, None])
    rank = jnp.sum(earlier.astype(jnp.int32), axis=1)
    return owner_of * slot_count + rank


def receive_slots(panel_list, owner_list, owner_count, own_index, slot_count):
    capacity = owner_list.shape[1]
    list_len = panel_list.shape[1]
    wanted = owner_list[own_index]
    live = jnp.arange(capacity, dtype=jnp.int32) < owner_count[own_index]
    match = (panel_list[:, :, None] == wanted[None, None, :]) & live[None, None, :]
    hit = jnp.any(match, axis=2)
    slot_of = jnp.sum(jnp.where(match, jnp.arange(capacity, dtype=jnp.int32)[None, None, :], 0), axis=2)
    position = jnp.arange(list_len, dtype=jnp.int32)
    earlier = hit[:, None, :] & (position[None, None, :] < position[None, :, None])
    rank = jnp.sum(earlier.astype(jnp.int32), axis=2)
    ranks = jnp.arange(slot_count, dtype=jnp.int32)
    chosen = hit[:, :, None] & (rank[:, :, None] == ranks[None, None, :])
    found = jnp.any(chosen, axis=1)
    dest = jnp.sum(jnp.where(chosen, slot_of[:, :, None], 0), axis=1)
    return jnp.where(found, dest, capacity).reshape(-1)


def project_kernel(sizes, kp, block_len, face_base, has_acc, pos_ref, pat_ref, p_ref, *refs):
    n = len(sizes)
    w_refs = refs[:n]
    if has_acc:
        acc_ref, o_ref, buf, sem = refs[n:]
        o_ref[...] = acc_ref[...]
    else:
        o_ref, buf, sem = refs[n:]
        o_ref[...] = jnp.zeros_like(o_ref)

    def fetch(q):
        slot = q % 2
        rows = sizes[q] * kp * block_len
        return pltpu.make_async_copy(
            w_refs[q].at[pl.ds(0, rows)], buf.at[slot, pl.ds(0, rows)], sem.at[slot]
        )

    copies = [fetch(0)]
    copies[0].start()
    base = 0
    for q in range(n):
        copies[q].wait()
        if q + 1 < n:
            copies.append(fetch(q + 1))
            copies[q + 1].start()
        slot = q % 2
        for g in range(sizes[q]):
            face = base + g
            col = face_base + face
            rows = p_ref[:, col * block_len:(col + 1) * block_len]
            wide = jnp.concatenate(
                [buf[slot, (g * kp + k) * block_len:(g * kp + k + 1) * block_len, :] for k in range(kp)],
                axis=1,
            )
            prod = jnp.dot(rows, wide, preferred_element_type=jnp.float32)
            for k in range(kp):
                pos = pos_ref[pat_ref[face * kp + k]]
                o_ref[pos] += prod[:, k * block_len:(k + 1) * block_len]
        base += sizes[q]


def project(positions, pat, pressure, pieces, sizes, kp, n_pos, face_base, acc):
    time_len, block_len = pressure.shape[0], pieces[0].shape[1]
    face_blocks = sum(sizes)
    has_acc = acc is not None
    extra = [acc] if has_acc else []
    return pl.pallas_call(
        functools.partial(project_kernel, tuple(sizes), kp, block_len, face_base, has_acc),
        out_shape=jax.ShapeDtypeStruct((n_pos, time_len, block_len), jnp.float32),
        in_specs=[
            pl.BlockSpec(memory_space=pltpu.SMEM),
            pl.BlockSpec(memory_space=pltpu.SMEM),
            pl.BlockSpec(memory_space=pltpu.VMEM),
        ]
        + [pl.BlockSpec(memory_space=pl.ANY)] * len(pieces)
        + [pl.BlockSpec(memory_space=pltpu.VMEM)] * len(extra),
        out_specs=pl.BlockSpec(memory_space=pltpu.VMEM),
        scratch_shapes=[
            pltpu.VMEM((2, max(sizes) * kp * block_len, block_len), pieces[0].dtype),
            pltpu.SemaphoreType.DMA((2,)),
        ],
        cost_estimate=pl.CostEstimate(
            flops=2 * face_blocks * kp * time_len * block_len * block_len,
            bytes_accessed=face_blocks * kp * block_len * block_len * 2 + pressure.size * 2
            + (1 + len(extra)) * n_pos * time_len * block_len * 4,
            transcendentals=0,
        ),
    )(positions, pat, pressure, *pieces, *extra)


def collect_kernel(n_rows, dest_ref, r_ref, o_ref):
    o_ref[...] = jnp.zeros_like(o_ref)
    capacity = o_ref.shape[0]

    def add_row(e, carry):
        d = dest_ref[e]

        @pl.when(d < capacity)
        def _():
            o_ref[d] += r_ref[e]

        return carry

    lax.fori_loop(0, n_rows, add_row, 0)


def collect(dest, received, capacity):
    n_rows, time_len, block_len = received.shape
    return pl.pallas_call(
        functools.partial(collect_kernel, n_rows),
        out_shape=jax.ShapeDtypeStruct((capacity, time_len, block_len), jnp.float32),
        in_specs=[
            pl.BlockSpec(memory_space=pltpu.SMEM),
            pl.BlockSpec(memory_space=pltpu.VMEM),
        ],
        out_specs=pl.BlockSpec(memory_space=pltpu.VMEM),
    )(dest, received)


def body(pressure, proj_weight, pattern, panel_list, owner_list, owner_count):
    owner_size = lax.axis_size("owner")
    own_index = lax.axis_index("owner")
    list_len = panel_list.shape[1]
    capacity = owner_list.shape[1]
    slot_count = max(2, list_len // owner_size)
    n_pos = owner_size * slot_count

    n_tm = lax.axis_size("tm")
    t = lax.axis_index("tm")
    fb_dev, kp, block_len = proj_weight.shape[1], proj_weight.shape[2], proj_weight.shape[3]
    half = fb_dev // 2
    w_rows = fb_dev * kp * block_len
    right = [(i, (i + 1) % n_tm) for i in range(n_tm)]
    left = [(i, (i - 1) % n_tm) for i in range(n_tm)]

    pat_row = jnp.zeros((1, block_len), proj_weight.dtype)
    pat_row = pat_row.at[0, : fb_dev * kp].set(pattern[0].reshape(-1).astype(proj_weight.dtype))
    own = jnp.concatenate([proj_weight[0].reshape(w_rows, block_len), pat_row], axis=0)

    x_r = x_l = own
    pieces, sizes, lane_at, order = [own], [fb_dev], [0], [t]
    for s in range(1, n_tm // 2):
        x_r = lax.ppermute(x_r, "tm", right)
        x_l = lax.ppermute(x_l, "tm", left)
        pieces += [x_r, x_l]
        sizes += [fb_dev, fb_dev]
        lane_at += [0, 0]
        order += [(t - s) % n_tm, (t + s) % n_tm]
    h_rows = half * kp * block_len
    h_r = lax.ppermute(jnp.concatenate([x_r[:h_rows], x_r[w_rows:]], axis=0), "tm", right)
    h_l = lax.ppermute(x_l[h_rows:], "tm", left)
    pieces += [h_r, h_l]
    sizes += [half, half]
    lane_at += [0, half * kp]
    order += [(t + n_tm // 2) % n_tm]

    positions = send_positions(panel_list, owner_list, owner_count, own_index, slot_count)
    time_len = pressure.shape[0]
    blocks = pressure.reshape(time_len, n_tm, fb_dev * block_len)
    ordered = jnp.take(blocks, jnp.stack(order), axis=1).reshape(time_len, -1)

    def pattern_of(group):
        rows = [pieces[i][-1, lane_at[i]:lane_at[i] + sizes[i] * kp] for i in group]
        return jnp.concatenate(rows).astype(jnp.int32)

    full = list(range(len(pieces) - 2))
    tail = [len(pieces) - 2, len(pieces) - 1]
    split = sum(sizes[i] for i in full) * block_len
    packed = project(positions, pattern_of(full), ordered[:, :split], [pieces[i] for i in full],
                     [sizes[i] for i in full], kp, n_pos, 0, None)
    packed = project(positions, pattern_of(tail), ordered[:, split:], [pieces[i] for i in tail],
                     [sizes[i] for i in tail], kp, n_pos, 0, packed)
    received = lax.all_to_all(packed, "owner", split_axis=0, concat_axis=0, tiled=True)
    dest = receive_slots(panel_list, owner_list, owner_count, own_index, slot_count)
    return collect(dest, received, capacity)


def solution(mesh):
    placed = (
        P("tm", "owner"),
        P("owner", "tm", None, None, None),
        P("owner", "tm", None),
        P(),
        P(),
        P(),
    )
    return jax.shard_map(
        body, mesh=mesh, in_specs=placed, out_specs=P("owner", "tm", None), check_vma=False
    )
```

```python
import functools

import jax
import jax.numpy as jnp
from jax import lax
from jax.experimental import pallas as pl
from jax.experimental.pallas import tpu as pltpu
from jax.sharding import PartitionSpec as P


def send_positions(panel_list, owner_list, owner_count, own_index, slot_count):
    owner_size, capacity = owner_list.shape
    row = panel_list[own_index]
    list_len = row.shape[0]
    live = jnp.arange(capacity, dtype=jnp.int32)[None, :] < owner_count[:, None]
    match = (row[:, None, None] == owner_list[None, :, :]) & live[None, :, :]
    owned_by = jnp.any(match, axis=2)
    owner_of = jnp.sum(jnp.where(owned_by, jnp.arange(owner_size, dtype=jnp.int32)[None, :], 0), axis=1)
    position = jnp.arange(list_len, dtype=jnp.int32)
    earlier = (owner_of[:, None] == owner_of[None, :]) & (position[None, :] < position[:, None])
    rank = jnp.sum(earlier.astype(jnp.int32), axis=1)
    return owner_of * slot_count + rank


def receive_slots(panel_list, owner_list, owner_count, own_index, slot_count):
    capacity = owner_list.shape[1]
    list_len = panel_list.shape[1]
    wanted = owner_list[own_index]
    live = jnp.arange(capacity, dtype=jnp.int32) < owner_count[own_index]
    match = (panel_list[:, :, None] == wanted[None, None, :]) & live[None, None, :]
    hit = jnp.any(match, axis=2)
    slot_of = jnp.sum(jnp.where(match, jnp.arange(capacity, dtype=jnp.int32)[None, None, :], 0), axis=2)
    position = jnp.arange(list_len, dtype=jnp.int32)
    earlier = hit[:, None, :] & (position[None, None, :] < position[None, :, None])
    rank = jnp.sum(earlier.astype(jnp.int32), axis=2)
    ranks = jnp.arange(slot_count, dtype=jnp.int32)
    chosen = hit[:, :, None] & (rank[:, :, None] == ranks[None, None, :])
    found = jnp.any(chosen, axis=1)
    dest = jnp.sum(jnp.where(chosen, slot_of[:, :, None], 0), axis=1)
    return jnp.where(found, dest, capacity).reshape(-1)


def project_kernel(sizes, kp, block_len, face_base, has_acc, pos_ref, pat_ref, p_ref, *refs):
    n = len(sizes)
    w_refs = refs[:n]
    if has_acc:
        acc_ref, o_ref, buf, sem = refs[n:]
        o_ref[...] = acc_ref[...]
    else:
        o_ref, buf, sem = refs[n:]
        o_ref[...] = jnp.zeros_like(o_ref)

    def fetch(q):
        slot = q % 2
        return pltpu.make_async_copy(w_refs[q], buf.at[slot, pl.ds(0, sizes[q])], sem.at[slot])

    copies = [fetch(0)]
    copies[0].start()
    base = 0
    for q in range(n):
        copies[q].wait()
        if q + 1 < n:
            copies.append(fetch(q + 1))
            copies[q + 1].start()
        slot = q % 2
        for g in range(sizes[q]):
            face = base + g
            col = face_base + face
            rows = p_ref[:, col * block_len:(col + 1) * block_len]
            wide = jnp.concatenate([buf[slot, g, k] for k in range(kp)], axis=1)
            prod = jnp.dot(rows, wide, preferred_element_type=jnp.float32)
            for k in range(kp):
                pos = pos_ref[pat_ref[face * kp + k]]
                o_ref[pos] += prod[:, k * block_len:(k + 1) * block_len]
        base += sizes[q]


def project(positions, pat, pressure, pieces, sizes, kp, n_pos, face_base, acc):
    time_len, block_len = pressure.shape[0], pieces[0].shape[-1]
    face_blocks = sum(sizes)
    has_acc = acc is not None
    extra = [acc] if has_acc else []
    return pl.pallas_call(
        functools.partial(project_kernel, tuple(sizes), kp, block_len, face_base, has_acc),
        out_shape=jax.ShapeDtypeStruct((n_pos, time_len, block_len), jnp.float32),
        in_specs=[
            pl.BlockSpec(memory_space=pltpu.SMEM),
            pl.BlockSpec(memory_space=pltpu.SMEM),
            pl.BlockSpec(memory_space=pltpu.VMEM),
        ]
        + [pl.BlockSpec(memory_space=pl.ANY)] * len(pieces)
        + [pl.BlockSpec(memory_space=pltpu.VMEM)] * len(extra),
        out_specs=pl.BlockSpec(memory_space=pltpu.VMEM),
        scratch_shapes=[
            pltpu.VMEM((2, max(sizes), kp, block_len, block_len), pieces[0].dtype),
            pltpu.SemaphoreType.DMA((2,)),
        ],
        cost_estimate=pl.CostEstimate(
            flops=2 * face_blocks * kp * time_len * block_len * block_len,
            bytes_accessed=face_blocks * kp * block_len * block_len * 2 + pressure.size * 2
            + (1 + len(extra)) * n_pos * time_len * block_len * 4,
            transcendentals=0,
        ),
    )(positions, pat, pressure, *pieces, *extra)


def collect_kernel(n_rows, dest_ref, r_ref, o_ref):
    o_ref[...] = jnp.zeros_like(o_ref)
    capacity = o_ref.shape[0]

    def add_row(e, carry):
        d = dest_ref[e]

        @pl.when(d < capacity)
        def _():
            o_ref[d] += r_ref[e]

        return carry

    lax.fori_loop(0, n_rows, add_row, 0)


def collect(dest, received, capacity):
    n_rows, time_len, block_len = received.shape
    return pl.pallas_call(
        functools.partial(collect_kernel, n_rows),
        out_shape=jax.ShapeDtypeStruct((capacity, time_len, block_len), jnp.float32),
        in_specs=[
            pl.BlockSpec(memory_space=pltpu.SMEM),
            pl.BlockSpec(memory_space=pltpu.VMEM),
        ],
        out_specs=pl.BlockSpec(memory_space=pltpu.VMEM),
    )(dest, received)


def body(pressure, proj_weight, pattern, panel_list, owner_list, owner_count):
    owner_size = lax.axis_size("owner")
    own_index = lax.axis_index("owner")
    list_len = panel_list.shape[1]
    capacity = owner_list.shape[1]
    slot_count = max(2, list_len // owner_size)
    n_pos = owner_size * slot_count

    n_tm = lax.axis_size("tm")
    t = lax.axis_index("tm")
    fb_dev, kp, block_len = proj_weight.shape[1], proj_weight.shape[2], proj_weight.shape[3]
    half = fb_dev // 2
    right = [(i, (i + 1) % n_tm) for i in range(n_tm)]
    left = [(i, (i - 1) % n_tm) for i in range(n_tm)]

    x_r = x_l = proj_weight[0]
    p_r = p_l = pattern[0]
    pieces, pats, sizes, order = [x_r], [p_r], [fb_dev], [t]
    for s in range(1, n_tm // 2):
        x_r, p_r = lax.ppermute((x_r, p_r), "tm", right)
        x_l, p_l = lax.ppermute((x_l, p_l), "tm", left)
        x_r, p_r, x_l, p_l = lax.optimization_barrier((x_r, p_r, x_l, p_l))
        pieces += [x_r, x_l]
        pats += [p_r, p_l]
        sizes += [fb_dev, fb_dev]
        order += [(t - s) % n_tm, (t + s) % n_tm]
    h_r, q_r = lax.ppermute((x_r[:half], p_r[:half]), "tm", right)
    h_l, q_l = lax.ppermute((x_l[half:], p_l[half:]), "tm", left)
    h_r, q_r, h_l, q_l = lax.optimization_barrier((h_r, q_r, h_l, q_l))
    pieces += [h_r, h_l]
    pats += [q_r, q_l]
    sizes += [half, half]
    order += [(t + n_tm // 2) % n_tm]

    positions = send_positions(panel_list, owner_list, owner_count, own_index, slot_count)
    time_len = pressure.shape[0]
    blocks = pressure.reshape(time_len, n_tm, fb_dev * block_len)
    ordered = jnp.take(blocks, jnp.stack(order), axis=1).reshape(time_len, -1)

    def pattern_of(group):
        return jnp.concatenate([pats[i].reshape(-1) for i in group]).astype(jnp.int32)

    full = list(range(len(pieces) - 2))
    tail = [len(pieces) - 2, len(pieces) - 1]
    split = sum(sizes[i] for i in full) * block_len
    packed = project(positions, pattern_of(full), ordered[:, :split], [pieces[i] for i in full],
                     [sizes[i] for i in full], kp, n_pos, 0, None)
    packed = project(positions, pattern_of(tail), ordered[:, split:], [pieces[i] for i in tail],
                     [sizes[i] for i in tail], kp, n_pos, 0, packed)
    received = lax.all_to_all(packed, "owner", split_axis=0, concat_axis=0, tiled=True)
    dest = receive_slots(panel_list, owner_list, owner_count, own_index, slot_count)
    return collect(dest, received, capacity)


def solution(mesh):
    placed = (
        P("tm", "owner"),
        P("owner", "tm", None, None, None),
        P("owner", "tm", None),
        P(),
        P(),
        P(),
    )
    return jax.shard_map(
        body, mesh=mesh, in_specs=placed, out_specs=P("owner", "tm", None), check_vma=False
    )
```

```python
import functools

import jax
import jax.numpy as jnp
from jax import lax
from jax.experimental import pallas as pl
from jax.experimental.pallas import tpu as pltpu
from jax.sharding import PartitionSpec as P


def send_positions(panel_list, owner_list, owner_count, own_index, slot_count):
    owner_size, capacity = owner_list.shape
    row = panel_list[own_index]
    list_len = row.shape[0]
    live = jnp.arange(capacity, dtype=jnp.int32)[None, :] < owner_count[:, None]
    match = (row[:, None, None] == owner_list[None, :, :]) & live[None, :, :]
    owned_by = jnp.any(match, axis=2)
    owner_of = jnp.sum(jnp.where(owned_by, jnp.arange(owner_size, dtype=jnp.int32)[None, :], 0), axis=1)
    position = jnp.arange(list_len, dtype=jnp.int32)
    earlier = (owner_of[:, None] == owner_of[None, :]) & (position[None, :] < position[:, None])
    rank = jnp.sum(earlier.astype(jnp.int32), axis=1)
    return owner_of * slot_count + rank


def receive_slots(panel_list, owner_list, owner_count, own_index, slot_count):
    capacity = owner_list.shape[1]
    list_len = panel_list.shape[1]
    wanted = owner_list[own_index]
    live = jnp.arange(capacity, dtype=jnp.int32) < owner_count[own_index]
    match = (panel_list[:, :, None] == wanted[None, None, :]) & live[None, None, :]
    hit = jnp.any(match, axis=2)
    slot_of = jnp.sum(jnp.where(match, jnp.arange(capacity, dtype=jnp.int32)[None, None, :], 0), axis=2)
    position = jnp.arange(list_len, dtype=jnp.int32)
    earlier = hit[:, None, :] & (position[None, None, :] < position[None, :, None])
    rank = jnp.sum(earlier.astype(jnp.int32), axis=2)
    ranks = jnp.arange(slot_count, dtype=jnp.int32)
    chosen = hit[:, :, None] & (rank[:, :, None] == ranks[None, None, :])
    found = jnp.any(chosen, axis=1)
    dest = jnp.sum(jnp.where(chosen, slot_of[:, :, None], 0), axis=1)
    return jnp.where(found, dest, capacity).reshape(-1)


def project_kernel(sizes, kp, block_len, face_base, has_acc, pos_ref, pat_ref, p_ref, *refs):
    n = len(sizes)
    w_refs = refs[:n]
    if has_acc:
        acc_ref, o_ref, buf, sem = refs[n:]
    else:
        o_ref, buf, sem = refs[n:]
    rows_of = [sizes[q] * kp * block_len for q in range(n)]
    copies = [
        pltpu.make_async_copy(w_refs[q].at[pl.ds(0, rows_of[q])], buf.at[q, pl.ds(0, rows_of[q])], sem.at[q])
        for q in range(n)
    ]
    for c in copies:
        c.start()
    if has_acc:
        o_ref[...] = acc_ref[...]
    else:
        o_ref[...] = jnp.zeros_like(o_ref)
    base = 0
    for q in range(n):
        copies[q].wait()
        slot = q
        for g in range(sizes[q]):
            face = base + g
            col = face_base + face
            rows = p_ref[:, col * block_len:(col + 1) * block_len]
            wide = jnp.concatenate(
                [buf[slot, (g * kp + k) * block_len:(g * kp + k + 1) * block_len, :] for k in range(kp)],
                axis=1,
            )
            prod = jnp.dot(rows, wide, preferred_element_type=jnp.float32)
            for k in range(kp):
                pos = pos_ref[pat_ref[face * kp + k]]
                o_ref[pos] += prod[:, k * block_len:(k + 1) * block_len]
        base += sizes[q]


def project(positions, pat, pressure, pieces, sizes, kp, n_pos, face_base, acc):
    time_len, block_len = pressure.shape[0], pieces[0].shape[1]
    face_blocks = sum(sizes)
    has_acc = acc is not None
    extra = [acc] if has_acc else []
    return pl.pallas_call(
        functools.partial(project_kernel, tuple(sizes), kp, block_len, face_base, has_acc),
        out_shape=jax.ShapeDtypeStruct((n_pos, time_len, block_len), jnp.float32),
        in_specs=[
            pl.BlockSpec(memory_space=pltpu.SMEM),
            pl.BlockSpec(memory_space=pltpu.SMEM),
            pl.BlockSpec(memory_space=pltpu.VMEM),
        ]
        + [pl.BlockSpec(memory_space=pl.ANY)] * len(pieces)
        + [pl.BlockSpec(memory_space=pltpu.VMEM)] * len(extra),
        out_specs=pl.BlockSpec(memory_space=pltpu.VMEM),
        scratch_shapes=[
            pltpu.VMEM((len(pieces), max(sizes) * kp * block_len, block_len), pieces[0].dtype),
            pltpu.SemaphoreType.DMA((len(pieces),)),
        ],
        cost_estimate=pl.CostEstimate(
            flops=2 * face_blocks * kp * time_len * block_len * block_len,
            bytes_accessed=face_blocks * kp * block_len * block_len * 2 + pressure.size * 2
            + (1 + len(extra)) * n_pos * time_len * block_len * 4,
            transcendentals=0,
        ),
    )(positions, pat, pressure, *pieces, *extra)


def collect_kernel(n_rows, dest_ref, r_ref, o_ref):
    o_ref[...] = jnp.zeros_like(o_ref)
    capacity = o_ref.shape[0]

    def add_row(e, carry):
        d = dest_ref[e]

        @pl.when(d < capacity)
        def _():
            o_ref[d] += r_ref[e]

        return carry

    lax.fori_loop(0, n_rows, add_row, 0)


def collect(dest, received, capacity):
    n_rows, time_len, block_len = received.shape
    return pl.pallas_call(
        functools.partial(collect_kernel, n_rows),
        out_shape=jax.ShapeDtypeStruct((capacity, time_len, block_len), jnp.float32),
        in_specs=[
            pl.BlockSpec(memory_space=pltpu.SMEM),
            pl.BlockSpec(memory_space=pltpu.VMEM),
        ],
        out_specs=pl.BlockSpec(memory_space=pltpu.VMEM),
    )(dest, received)


def body(pressure, proj_weight, pattern, panel_list, owner_list, owner_count):
    owner_size = lax.axis_size("owner")
    own_index = lax.axis_index("owner")
    list_len = panel_list.shape[1]
    capacity = owner_list.shape[1]
    slot_count = max(2, list_len // owner_size)
    n_pos = owner_size * slot_count

    n_tm = lax.axis_size("tm")
    t = lax.axis_index("tm")
    fb_dev, kp, block_len = proj_weight.shape[1], proj_weight.shape[2], proj_weight.shape[3]
    half = fb_dev // 2
    w_rows = fb_dev * kp * block_len
    right = [(i, (i + 1) % n_tm) for i in range(n_tm)]
    left = [(i, (i - 1) % n_tm) for i in range(n_tm)]

    pat_row = jnp.zeros((1, block_len), proj_weight.dtype)
    pat_row = pat_row.at[0, : fb_dev * kp].set(pattern[0].reshape(-1).astype(proj_weight.dtype))
    own = jnp.concatenate([proj_weight[0].reshape(w_rows, block_len), pat_row], axis=0)

    x_r = x_l = own
    pieces, sizes, lane_at, order = [own], [fb_dev], [0], [t]
    for s in range(1, n_tm // 2):
        x_r = lax.ppermute(x_r, "tm", right)
        x_l = lax.ppermute(x_l, "tm", left)
        pieces += [x_r, x_l]
        sizes += [fb_dev, fb_dev]
        lane_at += [0, 0]
        order += [(t - s) % n_tm, (t + s) % n_tm]
    h_rows = half * kp * block_len
    h_r = lax.ppermute(jnp.concatenate([x_r[:h_rows], x_r[w_rows:]], axis=0), "tm", right)
    h_l = lax.ppermute(x_l[h_rows:], "tm", left)
    pieces += [h_r, h_l]
    sizes += [half, half]
    lane_at += [0, half * kp]
    order += [(t + n_tm // 2) % n_tm]

    positions = send_positions(panel_list, owner_list, owner_count, own_index, slot_count)
    time_len = pressure.shape[0]
    blocks = pressure.reshape(time_len, n_tm, fb_dev * block_len)
    ordered = jnp.take(blocks, jnp.stack(order), axis=1).reshape(time_len, -1)

    def pattern_of(group):
        rows = [pieces[i][-1, lane_at[i]:lane_at[i] + sizes[i] * kp] for i in group]
        return jnp.concatenate(rows).astype(jnp.int32)

    full = list(range(len(pieces) - 2))
    tail = [len(pieces) - 2, len(pieces) - 1]
    split = sum(sizes[i] for i in full) * block_len
    packed = project(positions, pattern_of(full), ordered[:, :split], [pieces[i] for i in full],
                     [sizes[i] for i in full], kp, n_pos, 0, None)
    packed = project(positions, pattern_of(tail), ordered[:, split:], [pieces[i] for i in tail],
                     [sizes[i] for i in tail], kp, n_pos, 0, packed)
    received = lax.all_to_all(packed, "owner", split_axis=0, concat_axis=0, tiled=True)
    dest = receive_slots(panel_list, owner_list, owner_count, own_index, slot_count)
    return collect(dest, received, capacity)


def solution(mesh):
    placed = (
        P("tm", "owner"),
        P("owner", "tm", None, None, None),
        P("owner", "tm", None),
        P(),
        P(),
        P(),
    )
    return jax.shard_map(
        body, mesh=mesh, in_specs=placed, out_specs=P("owner", "tm", None), check_vma=False
    )
```

```python
import functools

import jax
import jax.numpy as jnp
from jax import lax
from jax.experimental import pallas as pl
from jax.experimental.pallas import tpu as pltpu
from jax.sharding import PartitionSpec as P


def send_positions(panel_list, owner_list, owner_count, own_index, slot_count):
    owner_size, capacity = owner_list.shape
    row = panel_list[own_index]
    list_len = row.shape[0]
    live = jnp.arange(capacity, dtype=jnp.int32)[None, :] < owner_count[:, None]
    match = (row[:, None, None] == owner_list[None, :, :]) & live[None, :, :]
    owned_by = jnp.any(match, axis=2)
    owner_of = jnp.sum(jnp.where(owned_by, jnp.arange(owner_size, dtype=jnp.int32)[None, :], 0), axis=1)
    position = jnp.arange(list_len, dtype=jnp.int32)
    earlier = (owner_of[:, None] == owner_of[None, :]) & (position[None, :] < position[:, None])
    rank = jnp.sum(earlier.astype(jnp.int32), axis=1)
    return owner_of * slot_count + rank


def receive_slots(panel_list, owner_list, owner_count, own_index, slot_count):
    capacity = owner_list.shape[1]
    list_len = panel_list.shape[1]
    wanted = owner_list[own_index]
    live = jnp.arange(capacity, dtype=jnp.int32) < owner_count[own_index]
    match = (panel_list[:, :, None] == wanted[None, None, :]) & live[None, None, :]
    hit = jnp.any(match, axis=2)
    slot_of = jnp.sum(jnp.where(match, jnp.arange(capacity, dtype=jnp.int32)[None, None, :], 0), axis=2)
    position = jnp.arange(list_len, dtype=jnp.int32)
    earlier = hit[:, None, :] & (position[None, None, :] < position[None, :, None])
    rank = jnp.sum(earlier.astype(jnp.int32), axis=2)
    ranks = jnp.arange(slot_count, dtype=jnp.int32)
    chosen = hit[:, :, None] & (rank[:, :, None] == ranks[None, None, :])
    found = jnp.any(chosen, axis=1)
    dest = jnp.sum(jnp.where(chosen, slot_of[:, :, None], 0), axis=1)
    return jnp.where(found, dest, capacity).reshape(-1)


def project_kernel(sizes, kp, block_len, face_base, has_acc, pos_ref, pat_ref, p_ref, *refs):
    n = len(sizes)
    w_refs = refs[:n]
    if has_acc:
        acc_ref, o_ref, buf, sem = refs[n:]
    else:
        o_ref, buf, sem = refs[n:]
    rows_of = [sizes[q] * kp * block_len for q in range(n)]
    copies = [
        pltpu.make_async_copy(w_refs[q].at[pl.ds(0, rows_of[q])], buf.at[q, pl.ds(0, rows_of[q])], sem.at[q])
        for q in range(n)
    ]
    for c in copies:
        c.start()
    if has_acc:
        o_ref[...] = acc_ref[...]
    else:
        o_ref[...] = jnp.zeros_like(o_ref)
    base = 0
    for q in range(n):
        copies[q].wait()
        slot = q
        for g in range(sizes[q]):
            face = base + g
            col = face_base + face
            rows = p_ref[:, col * block_len:(col + 1) * block_len]
            wide = jnp.concatenate(
                [buf[slot, (g * kp + k) * block_len:(g * kp + k + 1) * block_len, :] for k in range(kp)],
                axis=1,
            )
            prod = jnp.dot(rows, wide, preferred_element_type=jnp.float32)
            for k in range(kp):
                pos = pos_ref[pat_ref[face * kp + k]]
                o_ref[pos] += prod[:, k * block_len:(k + 1) * block_len]
        base += sizes[q]


def project(positions, pat, pressure, pieces, sizes, kp, n_pos, face_base, acc):
    time_len, block_len = pressure.shape[0], pieces[0].shape[1]
    face_blocks = sum(sizes)
    has_acc = acc is not None
    extra = [acc] if has_acc else []
    return pl.pallas_call(
        functools.partial(project_kernel, tuple(sizes), kp, block_len, face_base, has_acc),
        out_shape=jax.ShapeDtypeStruct((n_pos, time_len, block_len), jnp.float32),
        in_specs=[
            pl.BlockSpec(memory_space=pltpu.SMEM),
            pl.BlockSpec(memory_space=pltpu.SMEM),
            pl.BlockSpec(memory_space=pltpu.VMEM),
        ]
        + [pl.BlockSpec(memory_space=pl.ANY)] * len(pieces)
        + [pl.BlockSpec(memory_space=pltpu.VMEM)] * len(extra),
        out_specs=pl.BlockSpec(memory_space=pltpu.VMEM),
        scratch_shapes=[
            pltpu.VMEM((len(pieces), max(sizes) * kp * block_len, block_len), pieces[0].dtype),
            pltpu.SemaphoreType.DMA((len(pieces),)),
        ],
        cost_estimate=pl.CostEstimate(
            flops=2 * face_blocks * kp * time_len * block_len * block_len,
            bytes_accessed=face_blocks * kp * block_len * block_len * 2 + pressure.size * 2
            + (1 + len(extra)) * n_pos * time_len * block_len * 4,
            transcendentals=0,
        ),
    )(positions, pat, pressure, *pieces, *extra)


def collect_kernel(n_rows, n_chunks, dest_ref, r_hbm, o_ref, buf, sem):
    capacity = o_ref.shape[0]
    rows_per = n_rows // n_chunks
    copies = [
        pltpu.make_async_copy(r_hbm.at[pl.ds(c * rows_per, rows_per)], buf.at[c], sem.at[c])
        for c in range(n_chunks)
    ]
    for c in copies:
        c.start()
    o_ref[...] = jnp.zeros_like(o_ref)
    for c in range(n_chunks):
        copies[c].wait()

        def add_row(e, carry):
            d = dest_ref[c * rows_per + e]

            @pl.when(d < capacity)
            def _():
                o_ref[d] += buf[c, e]

            return carry

        lax.fori_loop(0, rows_per, add_row, 0)


def collect(dest, received, capacity, n_chunks=4):
    n_rows, time_len, block_len = received.shape
    return pl.pallas_call(
        functools.partial(collect_kernel, n_rows, n_chunks),
        out_shape=jax.ShapeDtypeStruct((capacity, time_len, block_len), jnp.float32),
        in_specs=[
            pl.BlockSpec(memory_space=pltpu.SMEM),
            pl.BlockSpec(memory_space=pl.ANY),
        ],
        out_specs=pl.BlockSpec(memory_space=pltpu.VMEM),
        scratch_shapes=[
            pltpu.VMEM((n_chunks, n_rows // n_chunks, time_len, block_len), jnp.float32),
            pltpu.SemaphoreType.DMA((n_chunks,)),
        ],
    )(dest, received)


def body(pressure, proj_weight, pattern, panel_list, owner_list, owner_count):
    owner_size = lax.axis_size("owner")
    own_index = lax.axis_index("owner")
    list_len = panel_list.shape[1]
    capacity = owner_list.shape[1]
    slot_count = max(2, list_len // owner_size)
    n_pos = owner_size * slot_count

    n_tm = lax.axis_size("tm")
    t = lax.axis_index("tm")
    fb_dev, kp, block_len = proj_weight.shape[1], proj_weight.shape[2], proj_weight.shape[3]
    half = fb_dev // 2
    w_rows = fb_dev * kp * block_len
    right = [(i, (i + 1) % n_tm) for i in range(n_tm)]
    left = [(i, (i - 1) % n_tm) for i in range(n_tm)]

    pat_row = jnp.pad(
        pattern[0].reshape(1, fb_dev * kp).astype(proj_weight.dtype), ((0, 0), (0, block_len - fb_dev * kp))
    )
    own = jnp.concatenate([proj_weight[0].reshape(w_rows, block_len), pat_row], axis=0)

    x_r = x_l = own
    pieces, sizes, lane_at, order = [own], [fb_dev], [0], [t]
    for s in range(1, n_tm // 2):
        x_r = lax.ppermute(x_r, "tm", right)
        x_l = lax.ppermute(x_l, "tm", left)
        pieces += [x_r, x_l]
        sizes += [fb_dev, fb_dev]
        lane_at += [0, 0]
        order += [(t - s) % n_tm, (t + s) % n_tm]
    h_rows = half * kp * block_len
    h_r = lax.ppermute(jnp.concatenate([x_r[:h_rows], x_r[w_rows:]], axis=0), "tm", right)
    h_l = lax.ppermute(x_l[h_rows:], "tm", left)
    pieces += [h_r, h_l]
    sizes += [half, half]
    lane_at += [0, half * kp]
    order += [(t + n_tm // 2) % n_tm]

    positions = send_positions(panel_list, owner_list, owner_count, own_index, slot_count)
    time_len = pressure.shape[0]
    blocks = pressure.reshape(time_len, n_tm, fb_dev * block_len)
    ordered = jnp.take(blocks, jnp.stack(order), axis=1).reshape(time_len, -1)

    def pattern_of(group):
        rows = [pieces[i][-1, lane_at[i]:lane_at[i] + sizes[i] * kp] for i in group]
        return jnp.concatenate(rows).astype(jnp.int32)

    full = list(range(len(pieces) - 2))
    tail = [len(pieces) - 2, len(pieces) - 1]
    split = sum(sizes[i] for i in full) * block_len
    packed = project(positions, pattern_of(full), ordered[:, :split], [pieces[i] for i in full],
                     [sizes[i] for i in full], kp, n_pos, 0, None)
    packed = project(positions, pattern_of(tail), ordered[:, split:], [pieces[i] for i in tail],
                     [sizes[i] for i in tail], kp, n_pos, 0, packed)
    received = lax.all_to_all(packed, "owner", split_axis=0, concat_axis=0, tiled=True)
    dest = receive_slots(panel_list, owner_list, owner_count, own_index, slot_count)
    return collect(dest, received, capacity)


def solution(mesh):
    placed = (
        P("tm", "owner"),
        P("owner", "tm", None, None, None),
        P("owner", "tm", None),
        P(),
        P(),
        P(),
    )
    return jax.shard_map(
        body, mesh=mesh, in_specs=placed, out_specs=P("owner", "tm", None), check_vma=False
    )
```

```python
import functools

import jax
import jax.numpy as jnp
from jax import lax
from jax.experimental import pallas as pl
from jax.experimental.pallas import tpu as pltpu
from jax.sharding import PartitionSpec as P


def send_positions(panel_list, owner_list, owner_count, own_index, slot_count):
    owner_size, capacity = owner_list.shape
    row = panel_list[own_index]
    list_len = row.shape[0]
    live = jnp.arange(capacity, dtype=jnp.int32)[None, :] < owner_count[:, None]
    match = (row[:, None, None] == owner_list[None, :, :]) & live[None, :, :]
    owned_by = jnp.any(match, axis=2)
    owner_of = jnp.sum(jnp.where(owned_by, jnp.arange(owner_size, dtype=jnp.int32)[None, :], 0), axis=1)
    position = jnp.arange(list_len, dtype=jnp.int32)
    earlier = (owner_of[:, None] == owner_of[None, :]) & (position[None, :] < position[:, None])
    rank = jnp.sum(earlier.astype(jnp.int32), axis=1)
    return owner_of * slot_count + rank


def receive_slots(panel_list, owner_list, owner_count, own_index, slot_count):
    capacity = owner_list.shape[1]
    list_len = panel_list.shape[1]
    wanted = owner_list[own_index]
    live = jnp.arange(capacity, dtype=jnp.int32) < owner_count[own_index]
    match = (panel_list[:, :, None] == wanted[None, None, :]) & live[None, None, :]
    hit = jnp.any(match, axis=2)
    slot_of = jnp.sum(jnp.where(match, jnp.arange(capacity, dtype=jnp.int32)[None, None, :], 0), axis=2)
    position = jnp.arange(list_len, dtype=jnp.int32)
    earlier = hit[:, None, :] & (position[None, None, :] < position[None, :, None])
    rank = jnp.sum(earlier.astype(jnp.int32), axis=2)
    ranks = jnp.arange(slot_count, dtype=jnp.int32)
    chosen = hit[:, :, None] & (rank[:, :, None] == ranks[None, None, :])
    found = jnp.any(chosen, axis=1)
    dest = jnp.sum(jnp.where(chosen, slot_of[:, :, None], 0), axis=1)
    return jnp.where(found, dest, capacity).reshape(-1)


def project_kernel(sizes, kp, block_len, face_base, has_acc, pos_ref, pat_ref, p_ref, *refs):
    n = len(sizes)
    w_refs = refs[:n]
    if has_acc:
        acc_hbm, o_ref, buf, sem = refs[n:]
    else:
        o_ref, buf, sem = refs[n:]
    rows_of = [sizes[q] * kp * block_len for q in range(n)]
    copies = [
        pltpu.make_async_copy(w_refs[q].at[pl.ds(0, rows_of[q])], buf.at[q, pl.ds(0, rows_of[q])], sem.at[q])
        for q in range(n)
    ]
    if has_acc:
        acc_copy = pltpu.make_async_copy(acc_hbm, o_ref, sem.at[n])
        acc_copy.start()
    for c in copies:
        c.start()
    if has_acc:
        acc_copy.wait()
    else:
        o_ref[...] = jnp.zeros_like(o_ref)
    base = 0
    for q in range(n):
        copies[q].wait()
        slot = q
        for g in range(sizes[q]):
            face = base + g
            col = face_base + face
            rows = p_ref[:, col * block_len:(col + 1) * block_len]
            wide = jnp.concatenate(
                [buf[slot, (g * kp + k) * block_len:(g * kp + k + 1) * block_len, :] for k in range(kp)],
                axis=1,
            )
            prod = jnp.dot(rows, wide, preferred_element_type=jnp.float32)
            for k in range(kp):
                pos = pos_ref[pat_ref[face * kp + k]]
                o_ref[pos] += prod[:, k * block_len:(k + 1) * block_len]
        base += sizes[q]


def project(positions, pat, pressure, pieces, sizes, kp, n_pos, face_base, acc):
    time_len, block_len = pressure.shape[0], pieces[0].shape[1]
    face_blocks = sum(sizes)
    has_acc = acc is not None
    extra = [acc] if has_acc else []
    return pl.pallas_call(
        functools.partial(project_kernel, tuple(sizes), kp, block_len, face_base, has_acc),
        out_shape=jax.ShapeDtypeStruct((n_pos, time_len, block_len), jnp.float32),
        in_specs=[
            pl.BlockSpec(memory_space=pltpu.SMEM),
            pl.BlockSpec(memory_space=pltpu.SMEM),
            pl.BlockSpec(memory_space=pltpu.VMEM),
        ]
        + [pl.BlockSpec(memory_space=pl.ANY)] * len(pieces)
        + [pl.BlockSpec(memory_space=pl.ANY)] * len(extra),
        out_specs=pl.BlockSpec(memory_space=pltpu.VMEM),
        scratch_shapes=[
            pltpu.VMEM((len(pieces), max(sizes) * kp * block_len, block_len), pieces[0].dtype),
            pltpu.SemaphoreType.DMA((len(pieces) + 1,)),
        ],
        cost_estimate=pl.CostEstimate(
            flops=2 * face_blocks * kp * time_len * block_len * block_len,
            bytes_accessed=face_blocks * kp * block_len * block_len * 2 + pressure.size * 2
            + (1 + len(extra)) * n_pos * time_len * block_len * 4,
            transcendentals=0,
        ),
    )(positions, pat, pressure, *pieces, *extra)


def collect_kernel(n_rows, n_chunks, dest_ref, r_hbm, o_ref, buf, sem):
    capacity = o_ref.shape[0]
    rows_per = n_rows // n_chunks
    copies = [
        pltpu.make_async_copy(r_hbm.at[pl.ds(c * rows_per, rows_per)], buf.at[c], sem.at[c])
        for c in range(n_chunks)
    ]
    for c in copies:
        c.start()
    o_ref[...] = jnp.zeros_like(o_ref)
    for c in range(n_chunks):
        copies[c].wait()

        for e in range(rows_per):
            d = dest_ref[c * rows_per + e]

            @pl.when(d < capacity)
            def _():
                o_ref[d] += buf[c, e]


def collect(dest, received, capacity, n_chunks=4):
    n_rows, time_len, block_len = received.shape
    return pl.pallas_call(
        functools.partial(collect_kernel, n_rows, n_chunks),
        out_shape=jax.ShapeDtypeStruct((capacity, time_len, block_len), jnp.float32),
        in_specs=[
            pl.BlockSpec(memory_space=pltpu.SMEM),
            pl.BlockSpec(memory_space=pl.ANY),
        ],
        out_specs=pl.BlockSpec(memory_space=pltpu.VMEM),
        scratch_shapes=[
            pltpu.VMEM((n_chunks, n_rows // n_chunks, time_len, block_len), jnp.float32),
            pltpu.SemaphoreType.DMA((n_chunks,)),
        ],
    )(dest, received)


def body(pressure, proj_weight, pattern, panel_list, owner_list, owner_count):
    owner_size = lax.axis_size("owner")
    own_index = lax.axis_index("owner")
    list_len = panel_list.shape[1]
    capacity = owner_list.shape[1]
    slot_count = max(2, list_len // owner_size)
    n_pos = owner_size * slot_count

    n_tm = lax.axis_size("tm")
    t = lax.axis_index("tm")
    fb_dev, kp, block_len = proj_weight.shape[1], proj_weight.shape[2], proj_weight.shape[3]
    half = fb_dev // 2
    w_rows = fb_dev * kp * block_len
    right = [(i, (i + 1) % n_tm) for i in range(n_tm)]
    left = [(i, (i - 1) % n_tm) for i in range(n_tm)]

    pat_row = jnp.pad(
        pattern[0].reshape(1, fb_dev * kp).astype(proj_weight.dtype), ((0, 0), (0, block_len - fb_dev * kp))
    )
    own = jnp.concatenate([proj_weight[0].reshape(w_rows, block_len), pat_row], axis=0)

    x_r = x_l = own
    pieces, sizes, lane_at, order = [own], [fb_dev], [0], [t]
    for s in range(1, n_tm // 2):
        x_r = lax.ppermute(x_r, "tm", right)
        x_l = lax.ppermute(x_l, "tm", left)
        pieces += [x_r, x_l]
        sizes += [fb_dev, fb_dev]
        lane_at += [0, 0]
        order += [(t - s) % n_tm, (t + s) % n_tm]
    h_rows = half * kp * block_len
    h_r = lax.ppermute(jnp.concatenate([x_r[:h_rows], x_r[w_rows:]], axis=0), "tm", right)
    h_l = lax.ppermute(x_l[h_rows:], "tm", left)
    pieces += [h_r, h_l]
    sizes += [half, half]
    lane_at += [0, half * kp]
    order += [(t + n_tm // 2) % n_tm]

    positions = send_positions(panel_list, owner_list, owner_count, own_index, slot_count)
    time_len = pressure.shape[0]
    blocks = pressure.reshape(time_len, n_tm, fb_dev * block_len)
    ordered = jnp.take(blocks, jnp.stack(order), axis=1).reshape(time_len, -1)

    def pattern_of(group):
        rows = [pieces[i][-1, lane_at[i]:lane_at[i] + sizes[i] * kp] for i in group]
        return jnp.concatenate(rows).astype(jnp.int32)

    full = list(range(len(pieces) - 2))
    tail = [len(pieces) - 2, len(pieces) - 1]
    split = sum(sizes[i] for i in full) * block_len
    packed = project(positions, pattern_of(full), ordered[:, :split], [pieces[i] for i in full],
                     [sizes[i] for i in full], kp, n_pos, 0, None)
    packed = project(positions, pattern_of(tail), ordered[:, split:], [pieces[i] for i in tail],
                     [sizes[i] for i in tail], kp, n_pos, 0, packed)
    received = lax.all_to_all(packed, "owner", split_axis=0, concat_axis=0, tiled=True)
    dest = receive_slots(panel_list, owner_list, owner_count, own_index, slot_count)
    return collect(dest, received, capacity)


def solution(mesh):
    placed = (
        P("tm", "owner"),
        P("owner", "tm", None, None, None),
        P("owner", "tm", None),
        P(),
        P(),
        P(),
    )
    return jax.shard_map(
        body, mesh=mesh, in_specs=placed, out_specs=P("owner", "tm", None), check_vma=False
    )
```

```python
import functools

import jax
import jax.numpy as jnp
from jax import lax
from jax.experimental import pallas as pl
from jax.experimental.pallas import tpu as pltpu
from jax.sharding import PartitionSpec as P


def send_positions(panel_list, owner_list, owner_count, own_index, slot_count):
    owner_size, capacity = owner_list.shape
    row = panel_list[own_index]
    list_len = row.shape[0]
    live = jnp.arange(capacity, dtype=jnp.int32)[None, :] < owner_count[:, None]
    match = (row[:, None, None] == owner_list[None, :, :]) & live[None, :, :]
    owned_by = jnp.any(match, axis=2)
    owner_of = jnp.sum(jnp.where(owned_by, jnp.arange(owner_size, dtype=jnp.int32)[None, :], 0), axis=1)
    position = jnp.arange(list_len, dtype=jnp.int32)
    earlier = (owner_of[:, None] == owner_of[None, :]) & (position[None, :] < position[:, None])
    rank = jnp.sum(earlier.astype(jnp.int32), axis=1)
    return owner_of * slot_count + rank


def receive_slots(panel_list, owner_list, owner_count, own_index, slot_count):
    capacity = owner_list.shape[1]
    list_len = panel_list.shape[1]
    wanted = owner_list[own_index]
    live = jnp.arange(capacity, dtype=jnp.int32) < owner_count[own_index]
    match = (panel_list[:, :, None] == wanted[None, None, :]) & live[None, None, :]
    hit = jnp.any(match, axis=2)
    slot_of = jnp.sum(jnp.where(match, jnp.arange(capacity, dtype=jnp.int32)[None, None, :], 0), axis=2)
    position = jnp.arange(list_len, dtype=jnp.int32)
    earlier = hit[:, None, :] & (position[None, None, :] < position[None, :, None])
    rank = jnp.sum(earlier.astype(jnp.int32), axis=2)
    ranks = jnp.arange(slot_count, dtype=jnp.int32)
    chosen = hit[:, :, None] & (rank[:, :, None] == ranks[None, None, :])
    found = jnp.any(chosen, axis=1)
    dest = jnp.sum(jnp.where(chosen, slot_of[:, :, None], 0), axis=1)
    return jnp.where(found, dest, capacity).reshape(-1)


def project_kernel(sizes, kp, block_len, face_base, has_acc, pos_ref, pat_ref, p_ref, *refs):
    n = len(sizes)
    w_refs = refs[:n]
    if has_acc:
        acc_hbm, o_ref, buf, sem = refs[n:]
    else:
        o_ref, buf, sem = refs[n:]
    rows_of = [sizes[q] * kp * block_len for q in range(n)]
    copies = [
        pltpu.make_async_copy(w_refs[q].at[pl.ds(0, rows_of[q])], buf.at[q, pl.ds(0, rows_of[q])], sem.at[q])
        for q in range(n)
    ]
    if has_acc:
        acc_copy = pltpu.make_async_copy(acc_hbm, o_ref, sem.at[n])
        acc_copy.start()
    for c in copies:
        c.start()
    if has_acc:
        acc_copy.wait()
    else:
        o_ref[...] = jnp.zeros_like(o_ref)
    base = 0
    for q in range(n):
        copies[q].wait()
        slot = q
        for g in range(sizes[q]):
            face = base + g
            col = face_base + face
            rows = p_ref[:, col * block_len:(col + 1) * block_len]
            wide = jnp.concatenate(
                [buf[slot, (g * kp + k) * block_len:(g * kp + k + 1) * block_len, :] for k in range(kp)],
                axis=1,
            )
            prod = jnp.dot(rows, wide, preferred_element_type=jnp.float32)
            for k in range(kp):
                pos = pos_ref[pat_ref[face * kp + k]]
                o_ref[pos] += prod[:, k * block_len:(k + 1) * block_len]
        base += sizes[q]


def project(positions, pat, pressure, pieces, sizes, kp, n_pos, face_base, acc):
    time_len, block_len = pressure.shape[0], pieces[0].shape[1]
    face_blocks = sum(sizes)
    has_acc = acc is not None
    extra = [acc] if has_acc else []
    return pl.pallas_call(
        functools.partial(project_kernel, tuple(sizes), kp, block_len, face_base, has_acc),
        out_shape=jax.ShapeDtypeStruct((n_pos, time_len, block_len), jnp.float32),
        in_specs=[
            pl.BlockSpec(memory_space=pltpu.SMEM),
            pl.BlockSpec(memory_space=pltpu.SMEM),
            pl.BlockSpec(memory_space=pltpu.VMEM),
        ]
        + [pl.BlockSpec(memory_space=pl.ANY)] * len(pieces)
        + [pl.BlockSpec(memory_space=pl.ANY)] * len(extra),
        out_specs=pl.BlockSpec(memory_space=pltpu.VMEM),
        scratch_shapes=[
            pltpu.VMEM((len(pieces), max(sizes) * kp * block_len, block_len), pieces[0].dtype),
            pltpu.SemaphoreType.DMA((len(pieces) + 1,)),
        ],
        cost_estimate=pl.CostEstimate(
            flops=2 * face_blocks * kp * time_len * block_len * block_len,
            bytes_accessed=face_blocks * kp * block_len * block_len * 2 + pressure.size * 2
            + (1 + len(extra)) * n_pos * time_len * block_len * 4,
            transcendentals=0,
        ),
    )(positions, pat, pressure, *pieces, *extra)


def collect_kernel(n_rows, n_chunks, dest_ref, r_hbm, o_ref, buf, sem):
    capacity = o_ref.shape[0]
    rows_per = n_rows // n_chunks
    copies = [
        pltpu.make_async_copy(r_hbm.at[pl.ds(c * rows_per, rows_per)], buf.at[c], sem.at[c])
        for c in range(n_chunks)
    ]
    for c in copies:
        c.start()
    o_ref[...] = jnp.zeros_like(o_ref)
    for c in range(n_chunks):
        copies[c].wait()

        for e in range(rows_per):
            d = dest_ref[c * rows_per + e]

            @pl.when(d < capacity)
            def _():
                o_ref[d] += buf[c, e]


def collect(dest, received, capacity, n_chunks=4):
    n_rows, time_len, block_len = received.shape
    return pl.pallas_call(
        functools.partial(collect_kernel, n_rows, n_chunks),
        out_shape=jax.ShapeDtypeStruct((capacity, time_len, block_len), jnp.float32),
        in_specs=[
            pl.BlockSpec(memory_space=pltpu.SMEM),
            pl.BlockSpec(memory_space=pl.ANY),
        ],
        out_specs=pl.BlockSpec(memory_space=pltpu.VMEM),
        scratch_shapes=[
            pltpu.VMEM((n_chunks, n_rows // n_chunks, time_len, block_len), jnp.float32),
            pltpu.SemaphoreType.DMA((n_chunks,)),
        ],
    )(dest, received)


def body(pressure, proj_weight, pattern, panel_list, owner_list, owner_count):
    owner_size = lax.axis_size("owner")
    own_index = lax.axis_index("owner")
    list_len = panel_list.shape[1]
    capacity = owner_list.shape[1]
    slot_count = max(2, list_len // owner_size)
    n_pos = owner_size * slot_count

    n_tm = lax.axis_size("tm")
    t = lax.axis_index("tm")
    fb_dev, kp, block_len = proj_weight.shape[1], proj_weight.shape[2], proj_weight.shape[3]
    half = fb_dev // 2
    w_rows = fb_dev * kp * block_len
    right = [(i, (i + 1) % n_tm) for i in range(n_tm)]
    left = [(i, (i - 1) % n_tm) for i in range(n_tm)]

    pat_row = jnp.pad(
        pattern[0].reshape(1, fb_dev * kp).astype(proj_weight.dtype), ((0, 0), (0, block_len - fb_dev * kp))
    )
    own = jnp.concatenate([proj_weight[0].reshape(w_rows, block_len), pat_row], axis=0)

    x_r = x_l = own
    pieces, sizes, lane_at, order = [own], [fb_dev], [0], [t]
    for s in range(1, n_tm // 2):
        x_r = lax.ppermute(x_r, "tm", right)
        x_l = lax.ppermute(x_l, "tm", left)
        pieces += [x_r, x_l]
        sizes += [fb_dev, fb_dev]
        lane_at += [0, 0]
        order += [(t - s) % n_tm, (t + s) % n_tm]
    h_rows = half * kp * block_len
    h_r = lax.ppermute(jnp.concatenate([x_r[:h_rows], x_r[w_rows:]], axis=0), "tm", right)
    h_l = lax.ppermute(x_l[h_rows:], "tm", left)
    pieces += [h_r, h_l]
    sizes += [half, half]
    lane_at += [0, half * kp]
    order += [(t + n_tm // 2) % n_tm]

    positions = send_positions(panel_list, owner_list, owner_count, own_index, slot_count)
    time_len = pressure.shape[0]
    blocks = pressure.reshape(time_len, n_tm, fb_dev * block_len)
    ordered = jnp.take(blocks, jnp.stack(order), axis=1).reshape(time_len, -1)

    def pattern_of(group):
        rows = [pieces[i][-1, lane_at[i]:lane_at[i] + sizes[i] * kp] for i in group]
        return jnp.concatenate(rows).astype(jnp.int32)

    full = list(range(len(pieces) - 2))
    tail = [len(pieces) - 2, len(pieces) - 1]
    split = sum(sizes[i] for i in full) * block_len
    packed = project(positions, pattern_of(full), ordered[:, :split], [pieces[i] for i in full],
                     [sizes[i] for i in full], kp, n_pos, 0, None)
    packed = project(positions, pattern_of(tail), ordered[:, split:], [pieces[i] for i in tail],
                     [sizes[i] for i in tail], kp, n_pos, 0, packed)
    received = lax.all_to_all(packed, "owner", split_axis=0, concat_axis=0, tiled=True)
    dest = receive_slots(panel_list, owner_list, owner_count, own_index, slot_count)
    slots = jnp.arange(capacity, dtype=jnp.int32)
    onehot = (slots[:, None] == dest[None, :]).astype(jnp.float32)
    return jnp.einsum(
        "ce,etb->ctb", onehot, received, precision=lax.Precision.HIGHEST, preferred_element_type=jnp.float32
    )


def solution(mesh):
    placed = (
        P("tm", "owner"),
        P("owner", "tm", None, None, None),
        P("owner", "tm", None),
        P(),
        P(),
        P(),
    )
    return jax.shard_map(
        body, mesh=mesh, in_specs=placed, out_specs=P("owner", "tm", None), check_vma=False
    )
```

```python
import functools

import jax
import jax.numpy as jnp
from jax import lax
from jax.experimental import pallas as pl
from jax.experimental.pallas import tpu as pltpu
from jax.sharding import PartitionSpec as P


def send_positions(panel_list, owner_list, owner_count, own_index, slot_count):
    owner_size, capacity = owner_list.shape
    row = panel_list[own_index]
    list_len = row.shape[0]
    live = jnp.arange(capacity, dtype=jnp.int32)[None, :] < owner_count[:, None]
    match = (row[:, None, None] == owner_list[None, :, :]) & live[None, :, :]
    owned_by = jnp.any(match, axis=2)
    owner_of = jnp.sum(jnp.where(owned_by, jnp.arange(owner_size, dtype=jnp.int32)[None, :], 0), axis=1)
    position = jnp.arange(list_len, dtype=jnp.int32)
    earlier = (owner_of[:, None] == owner_of[None, :]) & (position[None, :] < position[:, None])
    rank = jnp.sum(earlier.astype(jnp.int32), axis=1)
    return owner_of * slot_count + rank


def receive_slots(panel_list, owner_list, owner_count, own_index, slot_count):
    capacity = owner_list.shape[1]
    list_len = panel_list.shape[1]
    wanted = owner_list[own_index]
    live = jnp.arange(capacity, dtype=jnp.int32) < owner_count[own_index]
    match = (panel_list[:, :, None] == wanted[None, None, :]) & live[None, None, :]
    hit = jnp.any(match, axis=2)
    slot_of = jnp.sum(jnp.where(match, jnp.arange(capacity, dtype=jnp.int32)[None, None, :], 0), axis=2)
    position = jnp.arange(list_len, dtype=jnp.int32)
    earlier = hit[:, None, :] & (position[None, None, :] < position[None, :, None])
    rank = jnp.sum(earlier.astype(jnp.int32), axis=2)
    ranks = jnp.arange(slot_count, dtype=jnp.int32)
    chosen = hit[:, :, None] & (rank[:, :, None] == ranks[None, None, :])
    found = jnp.any(chosen, axis=1)
    dest = jnp.sum(jnp.where(chosen, slot_of[:, :, None], 0), axis=1)
    return jnp.where(found, dest, capacity).reshape(-1)


def project_kernel(sizes, kp, block_len, face_base, has_acc, pos_ref, pat_ref, p_ref, *refs):
    n = len(sizes)
    w_refs = refs[:n]
    if has_acc:
        acc_hbm, o_ref, buf, sem = refs[n:]
    else:
        o_ref, buf, sem = refs[n:]
    rows_of = [sizes[q] * kp * block_len for q in range(n)]
    copies = [
        pltpu.make_async_copy(w_refs[q].at[pl.ds(0, rows_of[q])], buf.at[q, pl.ds(0, rows_of[q])], sem.at[q])
        for q in range(n)
    ]
    if has_acc:
        acc_copy = pltpu.make_async_copy(acc_hbm, o_ref, sem.at[n])
        acc_copy.start()
    for c in copies:
        c.start()
    if has_acc:
        acc_copy.wait()
    else:
        o_ref[...] = jnp.zeros_like(o_ref)
    base = 0
    for q in range(n):
        copies[q].wait()
        slot = q
        for g in range(sizes[q]):
            face = base + g
            col = face_base + face
            rows = p_ref[:, col * block_len:(col + 1) * block_len]
            wide = jnp.concatenate(
                [buf[slot, (g * kp + k) * block_len:(g * kp + k + 1) * block_len, :] for k in range(kp)],
                axis=1,
            )
            prod = jnp.dot(rows, wide, preferred_element_type=jnp.float32)
            for k in range(kp):
                pos = pos_ref[pat_ref[face * kp + k]]
                o_ref[pos] += prod[:, k * block_len:(k + 1) * block_len]
        base += sizes[q]


def project(positions, pat, pressure, pieces, sizes, kp, n_pos, face_base, acc):
    time_len, block_len = pressure.shape[0], pieces[0].shape[1]
    face_blocks = sum(sizes)
    has_acc = acc is not None
    extra = [acc] if has_acc else []
    return pl.pallas_call(
        functools.partial(project_kernel, tuple(sizes), kp, block_len, face_base, has_acc),
        out_shape=jax.ShapeDtypeStruct((n_pos, time_len, block_len), jnp.float32),
        in_specs=[
            pl.BlockSpec(memory_space=pltpu.SMEM),
            pl.BlockSpec(memory_space=pltpu.SMEM),
            pl.BlockSpec(memory_space=pltpu.VMEM),
        ]
        + [pl.BlockSpec(memory_space=pl.ANY)] * len(pieces)
        + [pl.BlockSpec(memory_space=pl.ANY)] * len(extra),
        out_specs=pl.BlockSpec(memory_space=pltpu.VMEM),
        scratch_shapes=[
            pltpu.VMEM((len(pieces), max(sizes) * kp * block_len, block_len), pieces[0].dtype),
            pltpu.SemaphoreType.DMA((len(pieces) + 1,)),
        ],
        cost_estimate=pl.CostEstimate(
            flops=2 * face_blocks * kp * time_len * block_len * block_len,
            bytes_accessed=face_blocks * kp * block_len * block_len * 2 + pressure.size * 2
            + (1 + len(extra)) * n_pos * time_len * block_len * 4,
            transcendentals=0,
        ),
    )(positions, pat, pressure, *pieces, *extra)


def collect_kernel(n_rows, n_chunks, dest_ref, r_hbm, o_ref, buf, sem):
    capacity = o_ref.shape[0]
    rows_per = n_rows // n_chunks
    copies = [
        pltpu.make_async_copy(r_hbm.at[pl.ds(c * rows_per, rows_per)], buf.at[c], sem.at[c])
        for c in range(n_chunks)
    ]
    for c in copies:
        c.start()
    o_ref[...] = jnp.zeros_like(o_ref)
    for c in range(n_chunks):
        copies[c].wait()

        for e in range(rows_per):
            d = dest_ref[c * rows_per + e]

            @pl.when(d < capacity)
            def _():
                o_ref[d] += buf[c, e]


def collect(dest, received, capacity, n_chunks=4):
    n_rows, time_len, block_len = received.shape
    return pl.pallas_call(
        functools.partial(collect_kernel, n_rows, n_chunks),
        out_shape=jax.ShapeDtypeStruct((capacity, time_len, block_len), jnp.float32),
        in_specs=[
            pl.BlockSpec(memory_space=pltpu.SMEM),
            pl.BlockSpec(memory_space=pl.ANY),
        ],
        out_specs=pl.BlockSpec(memory_space=pltpu.VMEM),
        scratch_shapes=[
            pltpu.VMEM((n_chunks, n_rows // n_chunks, time_len, block_len), jnp.float32),
            pltpu.SemaphoreType.DMA((n_chunks,)),
        ],
    )(dest, received)


def body(pressure, proj_weight, pattern, panel_list, owner_list, owner_count):
    owner_size = lax.axis_size("owner")
    own_index = lax.axis_index("owner")
    list_len = panel_list.shape[1]
    capacity = owner_list.shape[1]
    slot_count = max(2, list_len // owner_size)
    n_pos = owner_size * slot_count

    n_tm = lax.axis_size("tm")
    t = lax.axis_index("tm")
    fb_dev, kp, block_len = proj_weight.shape[1], proj_weight.shape[2], proj_weight.shape[3]
    half = fb_dev // 2
    w_rows = fb_dev * kp * block_len
    right = [(i, (i + 1) % n_tm) for i in range(n_tm)]
    left = [(i, (i - 1) % n_tm) for i in range(n_tm)]

    pat_row = jnp.pad(
        pattern[0].reshape(1, fb_dev * kp).astype(proj_weight.dtype), ((0, 0), (0, block_len - fb_dev * kp))
    )
    own = jnp.concatenate([proj_weight[0].reshape(w_rows, block_len), pat_row], axis=0)

    x_r = x_l = own
    pieces, sizes, lane_at, order = [own], [fb_dev], [0], [t]
    for s in range(1, n_tm // 2):
        x_r = lax.ppermute(x_r, "tm", right)
        x_l = lax.ppermute(x_l, "tm", left)
        pieces += [x_r, x_l]
        sizes += [fb_dev, fb_dev]
        lane_at += [0, 0]
        order += [(t - s) % n_tm, (t + s) % n_tm]
    h_rows = half * kp * block_len
    h_r = lax.ppermute(jnp.concatenate([x_r[:h_rows], x_r[w_rows:]], axis=0), "tm", right)
    h_l = lax.ppermute(x_l[h_rows:], "tm", left)
    pieces += [h_r, h_l]
    sizes += [half, half]
    lane_at += [0, half * kp]
    order += [(t + n_tm // 2) % n_tm]

    positions = send_positions(panel_list, owner_list, owner_count, own_index, slot_count)
    time_len = pressure.shape[0]
    blocks = pressure.reshape(time_len, n_tm, fb_dev * block_len)
    ordered = jnp.take(blocks, jnp.stack(order), axis=1).reshape(time_len, -1)

    def pattern_of(group):
        rows = [pieces[i][-1, lane_at[i]:lane_at[i] + sizes[i] * kp] for i in group]
        return jnp.concatenate(rows).astype(jnp.int32)

    full = list(range(len(pieces) - 2))
    tail = [len(pieces) - 2, len(pieces) - 1]
    split = sum(sizes[i] for i in full) * block_len
    packed = project(positions, pattern_of(full), ordered[:, :split], [pieces[i] for i in full],
                     [sizes[i] for i in full], kp, n_pos, 0, None)
    packed = project(positions, pattern_of(tail), ordered[:, split:], [pieces[i] for i in tail],
                     [sizes[i] for i in tail], kp, n_pos, 0, packed)
    received = lax.all_to_all(packed, "owner", split_axis=0, concat_axis=0, tiled=True)
    dest = receive_slots(panel_list, owner_list, owner_count, own_index, slot_count)
    hi = lax.reduce_precision(received, exponent_bits=8, mantissa_bits=7)
    rest = received - hi
    mid = lax.reduce_precision(rest, exponent_bits=8, mantissa_bits=7)
    parts = jnp.concatenate([hi, mid, rest - mid], axis=0).astype(jnp.bfloat16)
    slots = jnp.arange(capacity, dtype=jnp.int32)
    onehot = (slots[:, None] == dest[None, :]).astype(jnp.bfloat16)
    onehot = jnp.concatenate([onehot] * 3, axis=1)
    return jnp.einsum("ce,etb->ctb", onehot, parts, preferred_element_type=jnp.float32)


def solution(mesh):
    placed = (
        P("tm", "owner"),
        P("owner", "tm", None, None, None),
        P("owner", "tm", None),
        P(),
        P(),
        P(),
    )
    return jax.shard_map(
        body, mesh=mesh, in_specs=placed, out_specs=P("owner", "tm", None), check_vma=False
    )
```

```python
import functools

import jax
import jax.numpy as jnp
from jax import lax
from jax.experimental import pallas as pl
from jax.experimental.pallas import tpu as pltpu
from jax.sharding import PartitionSpec as P


def send_positions(panel_list, owner_list, owner_count, own_index, slot_count):
    owner_size, capacity = owner_list.shape
    row = panel_list[own_index]
    list_len = row.shape[0]
    live = jnp.arange(capacity, dtype=jnp.int32)[None, :] < owner_count[:, None]
    match = (row[:, None, None] == owner_list[None, :, :]) & live[None, :, :]
    owned_by = jnp.any(match, axis=2)
    owner_of = jnp.sum(jnp.where(owned_by, jnp.arange(owner_size, dtype=jnp.int32)[None, :], 0), axis=1)
    position = jnp.arange(list_len, dtype=jnp.int32)
    earlier = (owner_of[:, None] == owner_of[None, :]) & (position[None, :] < position[:, None])
    rank = jnp.sum(earlier.astype(jnp.int32), axis=1)
    return owner_of * slot_count + rank


def receive_slots(panel_list, owner_list, owner_count, own_index, slot_count):
    capacity = owner_list.shape[1]
    list_len = panel_list.shape[1]
    wanted = owner_list[own_index]
    live = jnp.arange(capacity, dtype=jnp.int32) < owner_count[own_index]
    match = (panel_list[:, :, None] == wanted[None, None, :]) & live[None, None, :]
    hit = jnp.any(match, axis=2)
    slot_of = jnp.sum(jnp.where(match, jnp.arange(capacity, dtype=jnp.int32)[None, None, :], 0), axis=2)
    position = jnp.arange(list_len, dtype=jnp.int32)
    earlier = hit[:, None, :] & (position[None, None, :] < position[None, :, None])
    rank = jnp.sum(earlier.astype(jnp.int32), axis=2)
    ranks = jnp.arange(slot_count, dtype=jnp.int32)
    chosen = hit[:, :, None] & (rank[:, :, None] == ranks[None, None, :])
    found = jnp.any(chosen, axis=1)
    dest = jnp.sum(jnp.where(chosen, slot_of[:, :, None], 0), axis=1)
    return jnp.where(found, dest, capacity).reshape(-1)


def project_kernel(sizes, kp, block_len, face_base, has_acc, pos_ref, pat_ref, p_ref, *refs):
    n = len(sizes)
    w_refs = refs[:n]
    if has_acc:
        acc_hbm, o_ref, buf, sem = refs[n:]
    else:
        o_ref, buf, sem = refs[n:]
    rows_of = [sizes[q] * kp * block_len for q in range(n)]
    copies = [
        pltpu.make_async_copy(w_refs[q].at[pl.ds(0, rows_of[q])], buf.at[q, pl.ds(0, rows_of[q])], sem.at[q])
        for q in range(n)
    ]
    if has_acc:
        acc_copy = pltpu.make_async_copy(acc_hbm, o_ref, sem.at[n])
        acc_copy.start()
    for c in copies:
        c.start()
    if not has_acc:
        o_ref[...] = jnp.zeros_like(o_ref)
    base = 0
    for q in range(n):
        copies[q].wait()
        slot = q
        for g in range(sizes[q]):
            face = base + g
            col = face_base + face
            rows = p_ref[:, col * block_len:(col + 1) * block_len]
            wide = jnp.concatenate(
                [buf[slot, (g * kp + k) * block_len:(g * kp + k + 1) * block_len, :] for k in range(kp)],
                axis=1,
            )
            prod = jnp.dot(rows, wide, preferred_element_type=jnp.float32)
            if has_acc and face == 0:
                acc_copy.wait()
            for k in range(kp):
                pos = pos_ref[pat_ref[face * kp + k]]
                o_ref[pos] += prod[:, k * block_len:(k + 1) * block_len]
        base += sizes[q]


def project(positions, pat, pressure, pieces, sizes, kp, n_pos, face_base, acc):
    time_len, block_len = pressure.shape[0], pieces[0].shape[1]
    face_blocks = sum(sizes)
    has_acc = acc is not None
    extra = [acc] if has_acc else []
    return pl.pallas_call(
        functools.partial(project_kernel, tuple(sizes), kp, block_len, face_base, has_acc),
        out_shape=jax.ShapeDtypeStruct((n_pos, time_len, block_len), jnp.float32),
        in_specs=[
            pl.BlockSpec(memory_space=pltpu.SMEM),
            pl.BlockSpec(memory_space=pltpu.SMEM),
            pl.BlockSpec(memory_space=pltpu.VMEM),
        ]
        + [pl.BlockSpec(memory_space=pl.ANY)] * len(pieces)
        + [pl.BlockSpec(memory_space=pl.ANY)] * len(extra),
        out_specs=pl.BlockSpec(memory_space=pltpu.VMEM),
        scratch_shapes=[
            pltpu.VMEM((len(pieces), max(sizes) * kp * block_len, block_len), pieces[0].dtype),
            pltpu.SemaphoreType.DMA((len(pieces) + 1,)),
        ],
        cost_estimate=pl.CostEstimate(
            flops=2 * face_blocks * kp * time_len * block_len * block_len,
            bytes_accessed=face_blocks * kp * block_len * block_len * 2 + pressure.size * 2
            + (1 + len(extra)) * n_pos * time_len * block_len * 4,
            transcendentals=0,
        ),
    )(positions, pat, pressure, *pieces, *extra)


def collect_kernel(n_rows, n_chunks, dest_ref, r_hbm, o_ref, buf, sem):
    capacity = o_ref.shape[0]
    rows_per = n_rows // n_chunks
    copies = [
        pltpu.make_async_copy(r_hbm.at[pl.ds(c * rows_per, rows_per)], buf.at[c], sem.at[c])
        for c in range(n_chunks)
    ]
    for c in copies:
        c.start()
    o_ref[...] = jnp.zeros_like(o_ref)
    for c in range(n_chunks):
        copies[c].wait()

        for e in range(rows_per):
            d = dest_ref[c * rows_per + e]

            @pl.when(d < capacity)
            def _():
                o_ref[d] += buf[c, e]


def collect(dest, received, capacity, n_chunks=4):
    n_rows, time_len, block_len = received.shape
    return pl.pallas_call(
        functools.partial(collect_kernel, n_rows, n_chunks),
        out_shape=jax.ShapeDtypeStruct((capacity, time_len, block_len), jnp.float32),
        in_specs=[
            pl.BlockSpec(memory_space=pltpu.SMEM),
            pl.BlockSpec(memory_space=pl.ANY),
        ],
        out_specs=pl.BlockSpec(memory_space=pltpu.VMEM),
        scratch_shapes=[
            pltpu.VMEM((n_chunks, n_rows // n_chunks, time_len, block_len), jnp.float32),
            pltpu.SemaphoreType.DMA((n_chunks,)),
        ],
    )(dest, received)


def body(pressure, proj_weight, pattern, panel_list, owner_list, owner_count):
    owner_size = lax.axis_size("owner")
    own_index = lax.axis_index("owner")
    list_len = panel_list.shape[1]
    capacity = owner_list.shape[1]
    slot_count = max(2, list_len // owner_size)
    n_pos = owner_size * slot_count

    n_tm = lax.axis_size("tm")
    t = lax.axis_index("tm")
    fb_dev, kp, block_len = proj_weight.shape[1], proj_weight.shape[2], proj_weight.shape[3]
    half = fb_dev // 2
    w_rows = fb_dev * kp * block_len
    right = [(i, (i + 1) % n_tm) for i in range(n_tm)]
    left = [(i, (i - 1) % n_tm) for i in range(n_tm)]

    pat_row = jnp.pad(
        pattern[0].reshape(1, fb_dev * kp).astype(proj_weight.dtype), ((0, 0), (0, block_len - fb_dev * kp))
    )
    own = jnp.concatenate([proj_weight[0].reshape(w_rows, block_len), pat_row], axis=0)

    x_r = x_l = own
    pieces, sizes, lane_at, order = [own], [fb_dev], [0], [t]
    for s in range(1, n_tm // 2):
        x_r = lax.ppermute(x_r, "tm", right)
        x_l = lax.ppermute(x_l, "tm", left)
        pieces += [x_r, x_l]
        sizes += [fb_dev, fb_dev]
        lane_at += [0, 0]
        order += [(t - s) % n_tm, (t + s) % n_tm]
    h_rows = half * kp * block_len
    h_r = lax.ppermute(jnp.concatenate([x_r[:h_rows], x_r[w_rows:]], axis=0), "tm", right)
    h_l = lax.ppermute(x_l[h_rows:], "tm", left)
    pieces += [h_r, h_l]
    sizes += [half, half]
    lane_at += [0, half * kp]
    order += [(t + n_tm // 2) % n_tm]

    positions = send_positions(panel_list, owner_list, owner_count, own_index, slot_count)
    time_len = pressure.shape[0]
    blocks = pressure.reshape(time_len, n_tm, fb_dev * block_len)
    ordered = jnp.take(blocks, jnp.stack(order), axis=1).reshape(time_len, -1)

    def pattern_of(group):
        rows = [pieces[i][-1, lane_at[i]:lane_at[i] + sizes[i] * kp] for i in group]
        return jnp.concatenate(rows).astype(jnp.int32)

    full = list(range(len(pieces) - 2))
    tail = [len(pieces) - 2, len(pieces) - 1]
    split = sum(sizes[i] for i in full) * block_len
    packed = project(positions, pattern_of(full), ordered[:, :split], [pieces[i] for i in full],
                     [sizes[i] for i in full], kp, n_pos, 0, None)
    packed = project(positions, pattern_of(tail), ordered[:, split:], [pieces[i] for i in tail],
                     [sizes[i] for i in tail], kp, n_pos, 0, packed)
    received = lax.all_to_all(packed, "owner", split_axis=0, concat_axis=0, tiled=True)
    dest = receive_slots(panel_list, owner_list, owner_count, own_index, slot_count)
    slots = jnp.arange(capacity, dtype=jnp.int32)
    onehot = (slots[:, None] == dest[None, :]).astype(jnp.float32)
    return jnp.einsum(
        "ce,etb->ctb", onehot, received, precision=lax.Precision.HIGHEST, preferred_element_type=jnp.float32
    )


def solution(mesh):
    placed = (
        P("tm", "owner"),
        P("owner", "tm", None, None, None),
        P("owner", "tm", None),
        P(),
        P(),
        P(),
    )
    return jax.shard_map(
        body, mesh=mesh, in_specs=placed, out_specs=P("owner", "tm", None), check_vma=False
    )
```
